512 devices in a mesh: ctx: 32 (over y_hi, z), ch: 16 (over x, y_lo, core).
Axes of the slice: x: 4, y: 4 (y_hi: 2, y_lo: 2; y = y_hi * 2 + y_lo), z: 16, core: 2. Of those that a mesh axis runs over, the one named last changes fastest.
Arguments:
- tokens: bfloat16 [16384, 4096], P('ctx', 'ch'), may hold values from -6 to 6
- in_weight: bfloat16 [3, 4096, 4096], P(None, 'ctx', 'ch'), may hold values from -0.09375 to 0.09375
- short_taps: float32 [3, 3, 4096], P(None, None, 'ch'), may hold values from -3 to 3
- rates: float32 [4096, 16], P('ch'), may hold values from 3.0517578e-05 to 0.0333333333
- residues: float32 [4096, 16], P('ch'), may hold values from -0.4 to 0.4
- skip: float32 [4096], P('ch'), may hold values from -4 to 4
- out_weight: bfloat16 [4096, 4096], P('ch', 'ctx'), may hold values from -0.09375 to 0.09375
Outputs:
- mixed: bfloat16 [16384, 4096], P('ctx', 'ch')
The draws below stay inside these ranges and needn't reach their ends.
All inputs are finite; a program needn't handle non-finite values.
Results may differ from the reference program's by a relative error of at most 0.023.
Values may be sent and summed in bfloat16 or wider, within the bound.
No kernel may reach another device: no remote copies, remote signals or barrier semaphores. Data moves between devices by JAX's collectives and lax.ppermute only.
A program may use at most 64 MiB of HBM per device.

```python
import math
import jax
import jax.numpy as jnp
from jax import lax

D = 4096
MODES = 16
SHORT = 3
LENGTH = 16384
N_CH = 16


def rate_table(key):
    lowest = 0.5 / LENGTH
    highest = 1.0 / 30
    first = jax.random.fold_in(key, 0)
    table = jnp.exp(jax.random.uniform(first, (D, MODES), jnp.float32, math.log(lowest), math.log(highest)))
    return jnp.clip(table, lowest, highest)


def draw_rates(key, part):
    return rate_table(jax.random.fold_in(key, 7))


def draw_residues(key, part):
    table = rate_table(jax.random.fold_in(key, 7))
    noise = jnp.clip(jax.random.normal(jax.random.fold_in(key, 9), (D, MODES), jnp.float32), -3.0, 3.0)
    return noise * jnp.sqrt(1.0 - jnp.exp(-2.0 * table)) * 0.5


def steps_of(rng, dims, cuts, low, high):
    loudness = 1.0
    for position, blocks in cuts:
        steps = jax.random.uniform(jax.random.fold_in(jax.random.fold_in(rng, 6), position), (blocks,), jnp.float32, low / len(cuts), high / len(cuts))
        loudness = loudness * jnp.repeat(jnp.exp(steps), dims[position] // blocks).reshape((-1,) + (1,) * (len(dims) - 1 - position))
    return loudness


def gaussian(stream_key, extent, deviation, bound, cuts=(), dtype=jnp.bfloat16):
    drawn = deviation * jax.random.normal(stream_key, extent, jnp.float32)
    if cuts:
        drawn = drawn * steps_of(stream_key, extent, cuts, -0.22, 0.18)
    return jnp.clip(drawn, -bound, bound).astype(dtype)


def setup_inputs(seed: int = 0) -> dict:
    splits = jax.random.split(jax.random.key(seed), 8)
    return {
        "tokens": gaussian(splits[0], (LENGTH, D), 1.0, 6.0, ((0, 32), (1, 16))),
        "in_weight": gaussian(splits[1], (3, D, D), D ** -0.5, 0.09375, ((1, 32), (2, 16))),
        "short_taps": gaussian(splits[2], (SHORT, 3, D), 0.6, 3.0, ((2, 16),), jnp.float32),
        "rates": draw_rates(jax.random.fold_in(splits[7], 71), 0),
        "residues": draw_residues(jax.random.fold_in(splits[7], 71), 0),
        "skip": gaussian(splits[5], (D,), 1.0, 4.0, ((0, 16),), jnp.float32),
        "out_weight": gaussian(splits[6], (D, D), D ** -0.5, 0.09375, ((0, 16), (1, 32))),
    }


def reference(tokens, in_weight, short_taps, rates, residues, skip, out_weight):
    proj = jnp.stack([jnp.dot(tokens, in_weight[j], preferred_element_type=jnp.float32) for j in range(3)]).astype(jnp.bfloat16)
    widened = jnp.pad(proj.astype(jnp.float32), ((0, 0), (SHORT - 1, 0), (0, 0)))
    feats = jnp.zeros(proj.shape, jnp.float32)
    for i in range(SHORT):
        feats = feats + short_taps[i][:, None, :] * widened[:, SHORT - 1 - i:SHORT - 1 - i + LENGTH, :]
    query = feats[0]
    gated = (feats[1] * feats[2]).astype(jnp.bfloat16)
    gated = lax.optimization_barrier(gated).astype(jnp.float32)
    decay = jnp.exp(-rates)

    def advance(state, row):
        zrow, qrow = row
        state = decay * state + zrow[:, None]
        yrow = jnp.sum(residues * state, axis=1) + skip * zrow
        return state, (qrow * yrow).astype(jnp.bfloat16)

    start = jnp.zeros(rates.shape, jnp.float32)
    _, hidden = lax.scan(advance, start, (gated, query))
    group = D // N_CH
    total = jnp.zeros((LENGTH, D), jnp.float32)
    for g in range(N_CH):
        part = jnp.dot(hidden[:, g * group:(g + 1) * group], out_weight[g * group:(g + 1) * group], preferred_element_type=jnp.float32).astype(jnp.bfloat16)
        total = total + lax.optimization_barrier(part).astype(jnp.float32)
    return total.astype(jnp.bfloat16)
```

```python
import jax
import jax.numpy as jnp
import numpy as np
from jax import lax
from jax.sharding import Mesh
from jax.sharding import PartitionSpec as P

SHORT = 3
BLOCK = 64
CTX = ("yh", "z")
CH = ("x", "ylo", "core")


def passed_along(block, axis, count, distance):
    route = [(i - distance, i) for i in range(count) if i - distance >= 0]
    return lax.ppermute(block, axis, route)


def carried_in(final, rates, rows, count):
    incoming = passed_along(final, CTX, count, 1)
    shift = 1
    while shift < count:
        incoming = incoming + jnp.exp(-(shift * rows) * rates) * passed_along(incoming, CTX, count, shift)
        shift *= 2
    return incoming


def block_terms(values, rates, residues):
    length, width = values.shape
    blocks = length // BLOCK
    where_in = jnp.arange(BLOCK, dtype=jnp.float32)
    decay_in = jnp.exp(-where_in[:, None, None] * rates[None])
    impulse = jnp.sum(residues[None] * decay_in, axis=2)
    ii = lax.broadcasted_iota(jnp.int32, (BLOCK, BLOCK, BLOCK), 0)
    jj = lax.broadcasted_iota(jnp.int32, (BLOCK, BLOCK, BLOCK), 1)
    ll = lax.broadcasted_iota(jnp.int32, (BLOCK, BLOCK, BLOCK), 2)
    pick = (ii - jj == ll).astype(jnp.float32).reshape(BLOCK * BLOCK, BLOCK)
    toeplitz = jnp.dot(pick, impulse, precision=lax.Precision.HIGHEST).reshape(BLOCK, BLOCK, width)
    tails = decay_in[::-1]
    heads = residues[None] * decay_in * jnp.exp(-rates)[None]
    shaped = values.reshape(blocks, BLOCK, width)
    inner = jnp.einsum("ijc,bjc->bic", toeplitz, shaped, precision=lax.Precision.HIGHEST)
    ends = jnp.einsum("jcm,bjc->bcm", tails, shaped, precision=lax.Precision.HIGHEST)
    factor = jnp.broadcast_to(jnp.exp(-BLOCK * rates)[None], ends.shape)
    states, _ = lax.associative_scan(link_states, (ends, factor))
    starts = jnp.concatenate([jnp.zeros_like(states[:1]), states[:-1]], axis=0)
    offsets = jnp.exp(-(BLOCK * jnp.arange(blocks, dtype=jnp.float32))[:, None, None] * rates[None])
    return (inner, starts, states[-1], heads, offsets)


def link_states(earlier, later):
    return (later[0] + later[1] * earlier[0], earlier[1] * later[1])


def finish(inner, starts, heads, values, skip):
    carried = jnp.einsum("icm,bcm->bic", heads, starts, precision=lax.Precision.HIGHEST)
    return (inner + carried).reshape(values.shape) + skip[None] * values


def gathered_tokens(tokens):
    rows, width = tokens.shape
    parts = lax.all_gather(tokens, "x")
    parts = lax.all_gather(parts, "ylo")
    parts = lax.all_gather(parts, "core")
    return jnp.transpose(parts, (3, 2, 1, 0, 4)).reshape(rows, -1)


def scattered_terms(terms, sizes):
    rows, total = terms.shape
    x, ylo, core = sizes
    split = terms.reshape(rows, x, ylo, core, total // (x * ylo * core))
    split = lax.psum_scatter(split, "core", scatter_dimension=3, tiled=False)
    split = lax.psum_scatter(split, "ylo", scatter_dimension=2, tiled=False)
    split = lax.psum_scatter(split, "x", scatter_dimension=1, tiled=False)
    return split


def make_shards(count, sizes):
    def shards(tokens, in_weight, short_taps, rates, residues, skip, out_weight):
        rows = tokens.shape[0]
        width = in_weight.shape[2]
        whole = gathered_tokens(tokens)
        weight = lax.all_gather(in_weight, "z", axis=1, tiled=True)
        weight = lax.all_gather(weight, "yh", axis=1, tiled=True)
        proj = jnp.einsum("td,jdc->jtc", whole, weight, preferred_element_type=jnp.float32)
        proj = proj.astype(jnp.bfloat16)
        earlier = passed_along(proj[:, rows - (SHORT - 1) :, :], CTX, count, 1)
        widened = jnp.concatenate([earlier, proj], axis=1).astype(jnp.float32)
        feats = jnp.zeros((3, rows, width), jnp.float32)
        for i in range(SHORT):
            feats = (
                feats + short_taps[i][:, None, :] * widened[:, SHORT - 1 - i : SHORT - 1 - i + rows, :]
            )
        query = feats[0]
        gated = (feats[1] * feats[2]).astype(jnp.bfloat16)
        values = gated.astype(jnp.float32)
        inner, starts, final, heads, offsets = block_terms(values, rates, residues)
        incoming = carried_in(final, rates, rows, count)
        starts = starts + offsets * incoming[None]
        conv = finish(inner, starts, heads, values, skip)
        hidden = (query * conv).astype(jnp.bfloat16)
        out_w = lax.all_gather(out_weight, "z", axis=1, tiled=True)
        out_w = lax.all_gather(out_w, "yh", axis=1, tiled=True)
        terms = jnp.dot(hidden, out_w, preferred_element_type=jnp.float32)
        mixed = scattered_terms(terms.astype(jnp.bfloat16), sizes)
        return mixed.reshape(rows, -1)

    return shards


def solution(mesh):
    count = mesh.shape["ctx"]
    lanes = mesh.shape["ch"]
    sizes = (lanes // 4, 2, 2)
    fine = Mesh(mesh.devices.reshape(2, count // 2, *sizes), CTX + CH)
    placed = (
        P(CTX, CH),
        P(None, CTX, CH),
        P(None, None, CH),
        P(CH, None),
        P(CH, None),
        P(CH),
        P(CH, CTX),
    )
    return jax.shard_map(
        make_shards(count, sizes), mesh=fine, in_specs=placed, out_specs=P(CTX, CH), check_vma=False
    )
```

```python
import jax
import jax.numpy as jnp
import numpy as np
from jax import lax
from jax.sharding import Mesh
from jax.sharding import PartitionSpec as P

SHORT = 3
BLOCK = 64
CTX = ("yh", "z")
CH = "ch"


def passed_along(block, axis, count, distance):
    route = [(i - distance, i) for i in range(count) if i - distance >= 0]
    return lax.ppermute(block, axis, route)


def carried_in(final, rates, rows, count):
    incoming = passed_along(final, CTX, count, 1)
    shift = 1
    while shift < count:
        incoming = incoming + jnp.exp(-(shift * rows) * rates) * passed_along(incoming, CTX, count, shift)
        shift *= 2
    return incoming


def block_terms(values, rates, residues):
    length, width = values.shape
    blocks = length // BLOCK
    where_in = jnp.arange(BLOCK, dtype=jnp.float32)
    decay_in = jnp.exp(-where_in[:, None, None] * rates[None])
    impulse = jnp.sum(residues[None] * decay_in, axis=2)
    ii = lax.broadcasted_iota(jnp.int32, (BLOCK, BLOCK, BLOCK), 0)
    jj = lax.broadcasted_iota(jnp.int32, (BLOCK, BLOCK, BLOCK), 1)
    ll = lax.broadcasted_iota(jnp.int32, (BLOCK, BLOCK, BLOCK), 2)
    pick = (ii - jj == ll).astype(jnp.float32).reshape(BLOCK * BLOCK, BLOCK)
    toeplitz = jnp.dot(pick, impulse, precision=lax.Precision.HIGHEST).reshape(BLOCK, BLOCK, width)
    tails = decay_in[::-1]
    heads = residues[None] * decay_in * jnp.exp(-rates)[None]
    shaped = values.reshape(blocks, BLOCK, width)
    inner = jnp.einsum("ijc,bjc->bic", toeplitz, shaped, precision=lax.Precision.HIGHEST)
    ends = jnp.einsum("jcm,bjc->bcm", tails, shaped, precision=lax.Precision.HIGHEST)
    factor = jnp.broadcast_to(jnp.exp(-BLOCK * rates)[None], ends.shape)
    states, _ = lax.associative_scan(link_states, (ends, factor))
    starts = jnp.concatenate([jnp.zeros_like(states[:1]), states[:-1]], axis=0)
    offsets = jnp.exp(-(BLOCK * jnp.arange(blocks, dtype=jnp.float32))[:, None, None] * rates[None])
    return (inner, starts, states[-1], heads, offsets)


def link_states(earlier, later):
    return (later[0] + later[1] * earlier[0], earlier[1] * later[1])


def finish(inner, starts, heads, values, skip):
    carried = jnp.einsum("icm,bcm->bic", heads, starts, precision=lax.Precision.HIGHEST)
    return (inner + carried).reshape(values.shape) + skip[None] * values


def gathered_tokens(tokens, lanes):
    rows, width = tokens.shape
    copies = jnp.broadcast_to(tokens[None], (lanes, rows, width))
    parts = lax.all_to_all(copies, CH, 0, 0)
    return jnp.transpose(parts, (1, 0, 2)).reshape(rows, lanes * width)


def scattered_terms(terms, lanes):
    rows, total = terms.shape
    split = terms.reshape(rows, lanes, total // lanes)
    parts = lax.all_to_all(split, CH, 1, 1)
    return jnp.sum(parts.astype(jnp.float32), axis=1).astype(jnp.bfloat16)


def make_shards(count, lanes):
    def shards(tokens, in_weight, short_taps, rates, residues, skip, out_weight):
        rows = tokens.shape[0]
        width = in_weight.shape[2]
        whole = gathered_tokens(tokens, lanes)
        weight = lax.all_gather(in_weight, "yh", axis=1)
        weight = lax.all_gather(weight, "z", axis=2)
        weight = weight.reshape(3, -1, width)
        proj = jnp.einsum("td,jdc->jtc", whole, weight, preferred_element_type=jnp.float32)
        proj = proj.astype(jnp.bfloat16)
        earlier = passed_along(proj[:, rows - (SHORT - 1) :, :], CTX, count, 1)
        widened = jnp.concatenate([earlier, proj], axis=1).astype(jnp.float32)
        feats = jnp.zeros((3, rows, width), jnp.float32)
        for i in range(SHORT):
            feats = (
                feats + short_taps[i][:, None, :] * widened[:, SHORT - 1 - i : SHORT - 1 - i + rows, :]
            )
        query = feats[0]
        gated = (feats[1] * feats[2]).astype(jnp.bfloat16)
        values = gated.astype(jnp.float32)
        inner, starts, final, heads, offsets = block_terms(values, rates, residues)
        incoming = carried_in(final, rates, rows, count)
        starts = starts + offsets * incoming[None]
        conv = finish(inner, starts, heads, values, skip)
        hidden = (query * conv).astype(jnp.bfloat16)
        out_w = lax.all_gather(out_weight, "yh", axis=1)
        out_w = lax.all_gather(out_w, "z", axis=2)
        out_w = out_w.reshape(out_weight.shape[0], -1)
        terms = jnp.dot(hidden, out_w, preferred_element_type=jnp.float32)
        return scattered_terms(terms.astype(jnp.bfloat16), lanes)

    return shards


def solution(mesh):
    count = mesh.shape["ctx"]
    lanes = mesh.shape["ch"]
    fine = Mesh(mesh.devices.reshape(2, count // 2, lanes), CTX + (CH,))
    placed = (
        P(CTX, CH),
        P(None, CTX, CH),
        P(None, None, CH),
        P(CH, None),
        P(CH, None),
        P(CH),
        P(CH, CTX),
    )
    return jax.shard_map(
        make_shards(count, lanes), mesh=fine, in_specs=placed, out_specs=P(CTX, CH), check_vma=False
    )
```

```python
import jax
import jax.numpy as jnp
import numpy as np
from jax import lax
from jax.sharding import Mesh
from jax.sharding import PartitionSpec as P

SHORT = 3
BLOCK = 64
CTX = ("yh", "z")
CH = "ch"


def passed_along(block, axis, count, distance):
    route = [(i - distance, i) for i in range(count) if i - distance >= 0]
    return lax.ppermute(block, axis, route)


def carried_in(final, rates, rows, count):
    incoming = passed_along(final, CTX, count, 1)
    shift = 1
    while shift < count:
        incoming = incoming + jnp.exp(-(shift * rows) * rates) * passed_along(incoming, CTX, count, shift)
        shift *= 2
    return incoming


def block_terms(values, rates, residues):
    length, width = values.shape
    blocks = length // BLOCK
    where_in = jnp.arange(BLOCK, dtype=jnp.float32)
    decay_in = jnp.exp(-where_in[:, None, None] * rates[None])
    impulse = jnp.sum(residues[None] * decay_in, axis=2)
    ii = lax.broadcasted_iota(jnp.int32, (BLOCK, BLOCK, BLOCK), 0)
    jj = lax.broadcasted_iota(jnp.int32, (BLOCK, BLOCK, BLOCK), 1)
    ll = lax.broadcasted_iota(jnp.int32, (BLOCK, BLOCK, BLOCK), 2)
    pick = (ii - jj == ll).astype(jnp.float32).reshape(BLOCK * BLOCK, BLOCK)
    toeplitz = jnp.dot(pick, impulse, precision=lax.Precision.HIGHEST).reshape(BLOCK, BLOCK, width)
    tails = decay_in[::-1]
    heads = residues[None] * decay_in * jnp.exp(-rates)[None]
    shaped = values.reshape(blocks, BLOCK, width)
    inner = jnp.einsum("ijc,bjc->bic", toeplitz, shaped, precision=lax.Precision.HIGHEST)
    ends = jnp.einsum("jcm,bjc->bcm", tails, shaped, precision=lax.Precision.HIGHEST)
    factor = jnp.broadcast_to(jnp.exp(-BLOCK * rates)[None], ends.shape)
    states, _ = lax.associative_scan(link_states, (ends, factor))
    starts = jnp.concatenate([jnp.zeros_like(states[:1]), states[:-1]], axis=0)
    offsets = jnp.exp(-(BLOCK * jnp.arange(blocks, dtype=jnp.float32))[:, None, None] * rates[None])
    return (inner, starts, states[-1], heads, offsets)


def link_states(earlier, later):
    return (later[0] + later[1] * earlier[0], earlier[1] * later[1])


def finish(inner, starts, heads, values, skip):
    carried = jnp.einsum("icm,bcm->bic", heads, starts, precision=lax.Precision.HIGHEST)
    return (inner + carried).reshape(values.shape) + skip[None] * values


def gathered_tokens(tokens, lanes):
    rows, width = tokens.shape
    copies = jnp.broadcast_to(tokens[None], (lanes, rows, width))
    parts = lax.all_to_all(copies, CH, 0, 0)
    return jnp.transpose(parts, (1, 0, 2)).reshape(rows, lanes * width)


def scattered_terms(terms, lanes):
    rows, total = terms.shape
    split = terms.reshape(rows, lanes, total // lanes)
    parts = lax.all_to_all(split, CH, 1, 1)
    return jnp.sum(parts.astype(jnp.float32), axis=1).astype(jnp.bfloat16)


def make_shards(count, lanes):
    def shards(tokens, in_weight, short_taps, rates, residues, skip, out_weight):
        rows = tokens.shape[0]
        width = in_weight.shape[2]
        whole = lax.all_gather(tokens, CH, axis=1, tiled=True)
        copies = jnp.broadcast_to(in_weight[None], (count,) + in_weight.shape)
        weight = lax.all_to_all(copies, CTX, 0, 0)
        weight = jnp.transpose(weight, (1, 0, 2, 3)).reshape(3, -1, width)
        proj = jnp.einsum("td,jdc->jtc", whole, weight, preferred_element_type=jnp.float32)
        proj = proj.astype(jnp.bfloat16)
        earlier = passed_along(proj[:, rows - (SHORT - 1) :, :], CTX, count, 1)
        widened = jnp.concatenate([earlier, proj], axis=1).astype(jnp.float32)
        feats = jnp.zeros((3, rows, width), jnp.float32)
        for i in range(SHORT):
            feats = (
                feats + short_taps[i][:, None, :] * widened[:, SHORT - 1 - i : SHORT - 1 - i + rows, :]
            )
        query = feats[0]
        gated = (feats[1] * feats[2]).astype(jnp.bfloat16)
        values = gated.astype(jnp.float32)
        inner, starts, final, heads, offsets = block_terms(values, rates, residues)
        incoming = carried_in(final, rates, rows, count)
        starts = starts + offsets * incoming[None]
        conv = finish(inner, starts, heads, values, skip)
        hidden = (query * conv).astype(jnp.bfloat16)
        out_w = lax.all_gather(out_weight, "yh", axis=1)
        out_w = lax.all_gather(out_w, "z", axis=2)
        out_w = out_w.reshape(out_weight.shape[0], -1)
        terms = jnp.dot(hidden, out_w, preferred_element_type=jnp.float32)
        return scattered_terms(terms.astype(jnp.bfloat16), lanes)

    return shards


def solution(mesh):
    count = mesh.shape["ctx"]
    lanes = mesh.shape["ch"]
    fine = Mesh(mesh.devices.reshape(2, count // 2, lanes), CTX + (CH,))
    placed = (
        P(CTX, CH),
        P(None, CTX, CH),
        P(None, None, CH),
        P(CH, None),
        P(CH, None),
        P(CH),
        P(CH, CTX),
    )
    return jax.shard_map(
        make_shards(count, lanes), mesh=fine, in_specs=placed, out_specs=P(CTX, CH), check_vma=False
    )
```

```python
import jax
import jax.numpy as jnp
import numpy as np
from jax import lax
from jax.sharding import Mesh
from jax.sharding import PartitionSpec as P

SHORT = 3
BLOCK = 64
CTX = ("yh", "z")
CH = "ch"


def passed_along(block, axis, count, distance):
    route = [(i - distance, i) for i in range(count) if i - distance >= 0]
    return lax.ppermute(block, axis, route)


def carried_in(final, rates, rows, count):
    incoming = passed_along(final, CTX, count, 1)
    shift = 1
    while shift < count:
        incoming = incoming + jnp.exp(-(shift * rows) * rates) * passed_along(incoming, CTX, count, shift)
        shift *= 2
    return incoming


def block_terms(values, rates, residues):
    length, width = values.shape
    blocks = length // BLOCK
    where_in = jnp.arange(BLOCK, dtype=jnp.float32)
    decay_in = jnp.exp(-where_in[:, None, None] * rates[None])
    impulse = jnp.sum(residues[None] * decay_in, axis=2)
    ii = lax.broadcasted_iota(jnp.int32, (BLOCK, BLOCK, BLOCK), 0)
    jj = lax.broadcasted_iota(jnp.int32, (BLOCK, BLOCK, BLOCK), 1)
    ll = lax.broadcasted_iota(jnp.int32, (BLOCK, BLOCK, BLOCK), 2)
    pick = (ii - jj == ll).astype(jnp.float32).reshape(BLOCK * BLOCK, BLOCK)
    toeplitz = jnp.dot(pick, impulse, precision=lax.Precision.HIGHEST).reshape(BLOCK, BLOCK, width)
    tails = decay_in[::-1]
    heads = residues[None] * decay_in * jnp.exp(-rates)[None]
    shaped = values.reshape(blocks, BLOCK, width)
    inner = jnp.einsum("ijc,bjc->bic", toeplitz, shaped, precision=lax.Precision.HIGHEST)
    ends = jnp.einsum("jcm,bjc->bcm", tails, shaped, precision=lax.Precision.HIGHEST)
    factor = jnp.broadcast_to(jnp.exp(-BLOCK * rates)[None], ends.shape)
    states, _ = lax.associative_scan(link_states, (ends, factor))
    starts = jnp.concatenate([jnp.zeros_like(states[:1]), states[:-1]], axis=0)
    offsets = jnp.exp(-(BLOCK * jnp.arange(blocks, dtype=jnp.float32))[:, None, None] * rates[None])
    return (inner, starts, states[-1], heads, offsets)


def link_states(earlier, later):
    return (later[0] + later[1] * earlier[0], earlier[1] * later[1])


def finish(inner, starts, heads, values, skip):
    carried = jnp.einsum("icm,bcm->bic", heads, starts, precision=lax.Precision.HIGHEST)
    return (inner + carried).reshape(values.shape) + skip[None] * values


def gathered_tokens(tokens, lanes):
    rows, width = tokens.shape
    copies = jnp.broadcast_to(tokens[None], (lanes, rows, width))
    parts = lax.all_to_all(copies, CH, 0, 0)
    return jnp.transpose(parts, (1, 0, 2)).reshape(rows, lanes * width)


def scattered_terms(terms, lanes):
    rows, total = terms.shape
    split = terms.reshape(rows, lanes, total // lanes)
    parts = lax.all_to_all(split, CH, 1, 1)
    return jnp.sum(parts.astype(jnp.float32), axis=1).astype(jnp.bfloat16)


def make_shards(count, lanes):
    def shards(tokens, in_weight, short_taps, rates, residues, skip, out_weight):
        rows = tokens.shape[0]
        width = in_weight.shape[2]
        whole = gathered_tokens(tokens, lanes)

        def spread(part):
            part = lax.all_gather(part, "yh", axis=1)
            part = lax.all_gather(part, "z", axis=2)
            return part.reshape(part.shape[0], -1, part.shape[-1])

        def shortened(weight):
            proj = jnp.einsum("td,jdc->jtc", whole, weight, preferred_element_type=jnp.float32)
            proj = proj.astype(jnp.bfloat16)
            earlier = passed_along(proj[:, rows - (SHORT - 1) :, :], CTX, count, 1)
            return jnp.concatenate([earlier, proj], axis=1).astype(jnp.float32)

        def filtered(widened, taps):
            feats = jnp.zeros((widened.shape[0], rows, width), jnp.float32)
            for i in range(SHORT):
                feats = feats + taps[i][:, None, :] * widened[:, SHORT - 1 - i : SHORT - 1 - i + rows, :]
            return feats

        pair = spread(in_weight[1:])
        first, pair = lax.optimization_barrier((in_weight[:1], pair))
        feats = filtered(shortened(pair), short_taps[:, 1:])
        alone = spread(first)
        out_src, alone = lax.optimization_barrier((out_weight, alone))
        query = filtered(shortened(alone), short_taps[:, :1])[0]
        gated = (feats[0] * feats[1]).astype(jnp.bfloat16)
        values = gated.astype(jnp.float32)
        inner, starts, final, heads, offsets = block_terms(values, rates, residues)
        incoming = carried_in(final, rates, rows, count)
        starts = starts + offsets * incoming[None]
        conv = finish(inner, starts, heads, values, skip)
        hidden = (query * conv).astype(jnp.bfloat16)
        out_w = lax.all_gather(out_src, "yh", axis=1)
        out_w = lax.all_gather(out_w, "z", axis=2)
        out_w = out_w.reshape(out_weight.shape[0], -1)
        terms = jnp.dot(hidden, out_w, preferred_element_type=jnp.float32)
        return scattered_terms(terms.astype(jnp.bfloat16), lanes)

    return shards


def solution(mesh):
    count = mesh.shape["ctx"]
    lanes = mesh.shape["ch"]
    fine = Mesh(mesh.devices.reshape(2, count // 2, lanes), CTX + (CH,))
    placed = (
        P(CTX, CH),
        P(None, CTX, CH),
        P(None, None, CH),
        P(CH, None),
        P(CH, None),
        P(CH),
        P(CH, CTX),
    )
    return jax.shard_map(
        make_shards(count, lanes), mesh=fine, in_specs=placed, out_specs=P(CTX, CH), check_vma=False
    )
```

```python
import jax
import jax.numpy as jnp
import numpy as np
from jax import lax
from jax.sharding import Mesh
from jax.sharding import PartitionSpec as P

SHORT = 3
BLOCK = 64
CTX = ("yh", "z")
CH = "ch"


def passed_along(block, axis, count, distance):
    route = [(i - distance, i) for i in range(count) if i - distance >= 0]
    return lax.ppermute(block, axis, route)


def carried_in(final, rates, rows, count):
    incoming = passed_along(final, CTX, count, 1)
    shift = 1
    while shift < count:
        incoming = incoming + jnp.exp(-(shift * rows) * rates) * passed_along(incoming, CTX, count, shift)
        shift *= 2
    return incoming


def block_terms(values, rates, residues):
    length, width = values.shape
    blocks = length // BLOCK
    where_in = jnp.arange(BLOCK, dtype=jnp.float32)
    decay_in = jnp.exp(-where_in[:, None, None] * rates[None])
    impulse = jnp.sum(residues[None] * decay_in, axis=2)
    ii = lax.broadcasted_iota(jnp.int32, (BLOCK, BLOCK, BLOCK), 0)
    jj = lax.broadcasted_iota(jnp.int32, (BLOCK, BLOCK, BLOCK), 1)
    ll = lax.broadcasted_iota(jnp.int32, (BLOCK, BLOCK, BLOCK), 2)
    pick = (ii - jj == ll).astype(jnp.float32).reshape(BLOCK * BLOCK, BLOCK)
    toeplitz = jnp.dot(pick, impulse, precision=lax.Precision.HIGHEST).reshape(BLOCK, BLOCK, width)
    tails = decay_in[::-1]
    heads = residues[None] * decay_in * jnp.exp(-rates)[None]
    shaped = values.reshape(blocks, BLOCK, width)
    inner = jnp.einsum("ijc,bjc->bic", toeplitz, shaped, precision=lax.Precision.HIGHEST)
    ends = jnp.einsum("jcm,bjc->bcm", tails, shaped, precision=lax.Precision.HIGHEST)
    factor = jnp.broadcast_to(jnp.exp(-BLOCK * rates)[None], ends.shape)
    states, _ = lax.associative_scan(link_states, (ends, factor))
    starts = jnp.concatenate([jnp.zeros_like(states[:1]), states[:-1]], axis=0)
    offsets = jnp.exp(-(BLOCK * jnp.arange(blocks, dtype=jnp.float32))[:, None, None] * rates[None])
    return (inner, starts, states[-1], heads, offsets)


def link_states(earlier, later):
    return (later[0] + later[1] * earlier[0], earlier[1] * later[1])


def finish(inner, starts, heads, values, skip):
    carried = jnp.einsum("icm,bcm->bic", heads, starts, precision=lax.Precision.HIGHEST)
    return (inner + carried).reshape(values.shape) + skip[None] * values


def gathered_tokens(tokens, lanes):
    copies = jnp.tile(tokens, (1, lanes))
    return lax.all_to_all(copies, CH, 1, 1, tiled=True)


def scattered_terms(terms, lanes):
    rows, total = terms.shape
    split = terms.reshape(rows, lanes, total // lanes)
    parts = lax.all_to_all(split, CH, 1, 1)
    return jnp.sum(parts.astype(jnp.float32), axis=1).astype(jnp.bfloat16)


def make_shards(count, lanes):
    def shards(tokens, in_weight, short_taps, rates, residues, skip, out_weight):
        rows = tokens.shape[0]
        width = in_weight.shape[2]
        whole = gathered_tokens(tokens, lanes)

        def spread(part):
            part = lax.all_gather(part, "yh", axis=1)
            part = lax.all_gather(part, "z", axis=2)
            return part.reshape(part.shape[0], -1, part.shape[-1])

        def shortened(weight):
            proj = jnp.einsum("td,jdc->jtc", whole, weight, preferred_element_type=jnp.float32)
            proj = proj.astype(jnp.bfloat16)
            earlier = passed_along(proj[:, rows - (SHORT - 1) :, :], CTX, count, 1)
            return jnp.concatenate([earlier, proj], axis=1).astype(jnp.float32)

        def filtered(widened, taps):
            feats = jnp.zeros((widened.shape[0], rows, width), jnp.float32)
            for i in range(SHORT):
                feats = feats + taps[i][:, None, :] * widened[:, SHORT - 1 - i : SHORT - 1 - i + rows, :]
            return feats

        pair = spread(in_weight[1:])
        packed = jnp.concatenate([in_weight[0], out_weight.T], axis=1)[None]
        packed, pair = lax.optimization_barrier((packed, pair))
        feats = filtered(shortened(pair), short_taps[:, 1:])
        packed = spread(packed)[0]
        query = filtered(shortened(packed[None, :, :width]), short_taps[:, :1])[0]
        gated = (feats[0] * feats[1]).astype(jnp.bfloat16)
        values = gated.astype(jnp.float32)
        inner, starts, final, heads, offsets = block_terms(values, rates, residues)
        incoming = carried_in(final, rates, rows, count)
        starts = starts + offsets * incoming[None]
        conv = finish(inner, starts, heads, values, skip)
        hidden = (query * conv).astype(jnp.bfloat16)
        terms = jnp.einsum("tc,ec->te", hidden, packed[:, width:], preferred_element_type=jnp.float32)
        return scattered_terms(terms.astype(jnp.bfloat16), lanes)

    return shards


def solution(mesh):
    count = mesh.shape["ctx"]
    lanes = mesh.shape["ch"]
    fine = Mesh(mesh.devices.reshape(2, count // 2, lanes), CTX + (CH,))
    placed = (
        P(CTX, CH),
        P(None, CTX, CH),
        P(None, None, CH),
        P(CH, None),
        P(CH, None),
        P(CH),
        P(CH, CTX),
    )
    return jax.shard_map(
        make_shards(count, lanes), mesh=fine, in_specs=placed, out_specs=P(CTX, CH), check_vma=False
    )
```

```python
import jax
import jax.numpy as jnp
import numpy as np
from jax import lax
from jax.sharding import Mesh
from jax.sharding import PartitionSpec as P

SHORT = 3
BLOCK = 64
CTX = ("yh", "z")
CH = "ch"


def passed_along(block, axis, count, distance):
    route = [(i - distance, i) for i in range(count) if i - distance >= 0]
    return lax.ppermute(block, axis, route)


def carried_in(final, rates, rows, count):
    copies = jnp.broadcast_to(final[None], (count,) + final.shape)
    every = lax.all_to_all(copies, CTX, 0, 0)
    position = lax.axis_index(CTX)
    earlier = jnp.arange(count)
    gap = jnp.maximum(position - 1 - earlier, 0).astype(jnp.float32)
    weight = jnp.exp(-(gap[:, None, None] * rows) * rates[None])
    weight = jnp.where((earlier < position)[:, None, None], weight, 0.0)
    return jnp.sum(weight * every, axis=0)


def block_terms(values, rates, residues):
    length, width = values.shape
    blocks = length // BLOCK
    where_in = jnp.arange(BLOCK, dtype=jnp.float32)
    decay_in = jnp.exp(-where_in[:, None, None] * rates[None])
    impulse = jnp.sum(residues[None] * decay_in, axis=2)
    ii = lax.broadcasted_iota(jnp.int32, (BLOCK, BLOCK, BLOCK), 0)
    jj = lax.broadcasted_iota(jnp.int32, (BLOCK, BLOCK, BLOCK), 1)
    ll = lax.broadcasted_iota(jnp.int32, (BLOCK, BLOCK, BLOCK), 2)
    pick = (ii - jj == ll).astype(jnp.float32).reshape(BLOCK * BLOCK, BLOCK)
    toeplitz = jnp.dot(pick, impulse, precision=lax.Precision.HIGHEST).reshape(BLOCK, BLOCK, width)
    tails = decay_in[::-1]
    heads = residues[None] * decay_in * jnp.exp(-rates)[None]
    shaped = values.reshape(blocks, BLOCK, width)
    inner = jnp.einsum("ijc,bjc->bic", toeplitz, shaped, precision=lax.Precision.HIGHEST)
    ends = jnp.einsum("jcm,bjc->bcm", tails, shaped, precision=lax.Precision.HIGHEST)
    factor = jnp.broadcast_to(jnp.exp(-BLOCK * rates)[None], ends.shape)
    states, _ = lax.associative_scan(link_states, (ends, factor))
    starts = jnp.concatenate([jnp.zeros_like(states[:1]), states[:-1]], axis=0)
    offsets = jnp.exp(-(BLOCK * jnp.arange(blocks, dtype=jnp.float32))[:, None, None] * rates[None])
    return (inner, starts, states[-1], heads, offsets)


def link_states(earlier, later):
    return (later[0] + later[1] * earlier[0], earlier[1] * later[1])


def finish(inner, starts, heads, values, skip):
    carried = jnp.einsum("icm,bcm->bic", heads, starts, precision=lax.Precision.HIGHEST)
    return (inner + carried).reshape(values.shape) + skip[None] * values


def gathered_tokens(tokens, lanes):
    copies = jnp.broadcast_to(tokens[:, None], (tokens.shape[0], lanes, tokens.shape[1]))
    return lax.all_to_all(copies, CH, 1, 1)


def scattered_terms(terms, lanes):
    rows, total = terms.shape
    split = terms.reshape(rows, lanes, total // lanes)
    parts = lax.all_to_all(split, CH, 1, 1)
    return jnp.sum(parts.astype(jnp.float32), axis=1).astype(jnp.bfloat16)


def make_shards(count, lanes):
    def shards(tokens, in_weight, short_taps, rates, residues, skip, out_weight):
        rows = tokens.shape[0]
        width = in_weight.shape[2]
        whole = gathered_tokens(tokens, lanes)

        def spread(part):
            part = lax.all_gather(part, "yh", axis=1)
            part = lax.all_gather(part, "z", axis=2)
            return part.reshape(part.shape[0], -1, part.shape[-1])

        def shortened(weight):
            weight = weight.reshape(weight.shape[0], lanes, -1, weight.shape[-1])
            proj = jnp.einsum("tkd,jkdc->jtc", whole, weight, preferred_element_type=jnp.float32)
            proj = proj.astype(jnp.bfloat16)
            earlier = passed_along(proj[:, rows - (SHORT - 1) :, :], CTX, count, 1)
            return jnp.concatenate([earlier, proj], axis=1).astype(jnp.float32)

        def filtered(widened, taps):
            feats = jnp.zeros((widened.shape[0], rows, width), jnp.float32)
            for i in range(SHORT):
                feats = feats + taps[i][:, None, :] * widened[:, SHORT - 1 - i : SHORT - 1 - i + rows, :]
            return feats

        pair = spread(in_weight[1:])
        packed = jnp.concatenate([in_weight[0], out_weight.T], axis=1)[None]
        packed, pair = lax.optimization_barrier((packed, pair))
        feats = filtered(shortened(pair), short_taps[:, 1:])
        packed = spread(packed)[0]
        query = filtered(shortened(packed[None, :, :width]), short_taps[:, :1])[0]
        gated = (feats[0] * feats[1]).astype(jnp.bfloat16)
        values = gated.astype(jnp.float32)
        inner, starts, final, heads, offsets = block_terms(values, rates, residues)
        incoming = carried_in(final, rates, rows, count)
        starts = starts + offsets * incoming[None]
        conv = finish(inner, starts, heads, values, skip)
        hidden = (query * conv).astype(jnp.bfloat16)
        terms = jnp.einsum("tc,ec->te", hidden, packed[:, width:], preferred_element_type=jnp.float32)
        return scattered_terms(terms.astype(jnp.bfloat16), lanes)

    return shards


def solution(mesh):
    count = mesh.shape["ctx"]
    lanes = mesh.shape["ch"]
    fine = Mesh(mesh.devices.reshape(2, count // 2, lanes), CTX + (CH,))
    placed = (
        P(CTX, CH),
        P(None, CTX, CH),
        P(None, None, CH),
        P(CH, None),
        P(CH, None),
        P(CH),
        P(CH, CTX),
    )
    return jax.shard_map(
        make_shards(count, lanes), mesh=fine, in_specs=placed, out_specs=P(CTX, CH), check_vma=False
    )
```

```python
import jax
import jax.numpy as jnp
import numpy as np
from jax import lax
from jax.sharding import Mesh
from jax.sharding import PartitionSpec as P

SHORT = 3
BLOCK = 64
CTX = ("yh", "z")
CH = "ch"


def passed_along(block, axis, count, distance):
    route = [(i - distance, i) for i in range(count) if i - distance >= 0]
    return lax.ppermute(block, axis, route)


def carried_in(final, rates, rows, count):
    copies = jnp.broadcast_to(final[None], (count,) + final.shape)
    every = lax.all_to_all(copies, CTX, 0, 0)
    position = lax.axis_index(CTX)
    earlier = jnp.arange(count)
    gap = jnp.maximum(position - 1 - earlier, 0).astype(jnp.float32)
    weight = jnp.exp(-(gap[:, None, None] * rows) * rates[None])
    weight = jnp.where((earlier < position)[:, None, None], weight, 0.0)
    return jnp.sum(weight * every, axis=0)


def block_terms(values, rates, residues):
    length, width = values.shape
    blocks = length // BLOCK
    where_in = jnp.arange(BLOCK, dtype=jnp.float32)
    decay_in = jnp.exp(-where_in[:, None, None] * rates[None])
    impulse = jnp.sum(residues[None] * decay_in, axis=2)
    ii = lax.broadcasted_iota(jnp.int32, (BLOCK, BLOCK, BLOCK), 0)
    jj = lax.broadcasted_iota(jnp.int32, (BLOCK, BLOCK, BLOCK), 1)
    ll = lax.broadcasted_iota(jnp.int32, (BLOCK, BLOCK, BLOCK), 2)
    pick = (ii - jj == ll).astype(jnp.float32).reshape(BLOCK * BLOCK, BLOCK)
    toeplitz = jnp.dot(pick, impulse, precision=lax.Precision.HIGHEST).reshape(BLOCK, BLOCK, width)
    tails = decay_in[::-1]
    heads = residues[None] * decay_in * jnp.exp(-rates)[None]
    shaped = values.reshape(blocks, BLOCK, width)
    inner = jnp.einsum("ijc,bjc->bic", toeplitz, shaped, precision=lax.Precision.HIGHEST)
    ends = jnp.einsum("jcm,bjc->bcm", tails, shaped, precision=lax.Precision.HIGHEST)
    factor = jnp.broadcast_to(jnp.exp(-BLOCK * rates)[None], ends.shape)
    states, _ = lax.associative_scan(link_states, (ends, factor))
    starts = jnp.concatenate([jnp.zeros_like(states[:1]), states[:-1]], axis=0)
    offsets = jnp.exp(-(BLOCK * jnp.arange(blocks, dtype=jnp.float32))[:, None, None] * rates[None])
    return (inner, starts, states[-1], heads, offsets)


def link_states(earlier, later):
    return (later[0] + later[1] * earlier[0], earlier[1] * later[1])


def finish(inner, starts, heads, values, skip):
    carried = jnp.einsum("icm,bcm->bic", heads, starts, precision=lax.Precision.HIGHEST)
    return (inner + carried).reshape(values.shape) + skip[None] * values


def gathered_tokens(tokens, lanes):
    copies = jnp.broadcast_to(tokens[:, None], (tokens.shape[0], lanes, tokens.shape[1]))
    return lax.all_to_all(copies, CH, 1, 1)


def scattered_terms(terms, lanes):
    rows, total = terms.shape
    split = terms.reshape(rows, lanes, total // lanes)
    parts = lax.all_to_all(split, CH, 1, 1)
    return jnp.sum(parts.astype(jnp.float32), axis=1).astype(jnp.bfloat16)


def make_shards(count, lanes):
    def shards(tokens, in_weight, short_taps, rates, residues, skip, out_weight):
        rows = tokens.shape[0]
        width = in_weight.shape[2]
        whole = gathered_tokens(tokens, lanes)
        halo = passed_along(whole[rows - (SHORT - 1) :], CTX, count, 1)

        def across_yh(part):
            return lax.all_gather(part, "yh", axis=1)

        def across_z(part):
            part = lax.all_gather(part, "z", axis=2)
            return part.reshape(part.shape[0], -1, part.shape[-1])

        def shortened(weight):
            weight = weight.reshape(weight.shape[0], lanes, -1, weight.shape[-1])
            proj = jnp.einsum("tkd,jkdc->jtc", whole, weight, preferred_element_type=jnp.float32)
            earlier = jnp.einsum("tkd,jkdc->jtc", halo, weight, preferred_element_type=jnp.float32)
            proj = jnp.concatenate([earlier, proj], axis=1).astype(jnp.bfloat16)
            return proj.astype(jnp.float32)

        def filtered(widened, taps):
            feats = jnp.zeros((widened.shape[0], rows, width), jnp.float32)
            for i in range(SHORT):
                feats = feats + taps[i][:, None, :] * widened[:, SHORT - 1 - i : SHORT - 1 - i + rows, :]
            return feats

        pair = across_z(across_yh(in_weight[1:]))
        packed = across_yh(jnp.concatenate([in_weight[0], out_weight.T], axis=1)[None])
        packed, pair = lax.optimization_barrier((packed, pair))
        feats = filtered(shortened(pair), short_taps[:, 1:])
        packed = across_z(packed)[0]
        query = filtered(shortened(packed[None, :, :width]), short_taps[:, :1])[0]
        gated = (feats[0] * feats[1]).astype(jnp.bfloat16)
        values = gated.astype(jnp.float32)
        inner, starts, final, heads, offsets = block_terms(values, rates, residues)
        incoming = carried_in(final, rates, rows, count)
        starts = starts + offsets * incoming[None]
        conv = finish(inner, starts, heads, values, skip)
        hidden = (query * conv).astype(jnp.bfloat16)
        terms = jnp.einsum("tc,ec->te", hidden, packed[:, width:], preferred_element_type=jnp.float32)
        return scattered_terms(terms.astype(jnp.bfloat16), lanes)

    return shards


def solution(mesh):
    count = mesh.shape["ctx"]
    lanes = mesh.shape["ch"]
    fine = Mesh(mesh.devices.reshape(2, count // 2, lanes), CTX + (CH,))
    placed = (
        P(CTX, CH),
        P(None, CTX, CH),
        P(None, None, CH),
        P(CH, None),
        P(CH, None),
        P(CH),
        P(CH, CTX),
    )
    return jax.shard_map(
        make_shards(count, lanes), mesh=fine, in_specs=placed, out_specs=P(CTX, CH), check_vma=False
    )
```

```python
import jax
import jax.numpy as jnp
import numpy as np
from jax import lax
from jax.sharding import Mesh
from jax.sharding import PartitionSpec as P

SHORT = 3
BLOCK = 64
CTX = ("yh", "z")
CH = "ch"


def passed_along(block, axis, count, distance):
    route = [(i - distance, i) for i in range(count) if i - distance >= 0]
    return lax.ppermute(block, axis, route)


def carried_in(final, rates, rows, count):
    copies = jnp.broadcast_to(final[None], (count,) + final.shape)
    every = lax.all_to_all(copies, CTX, 0, 0)
    position = lax.axis_index(CTX)
    earlier = jnp.arange(count)
    gap = jnp.maximum(position - 1 - earlier, 0).astype(jnp.float32)
    weight = jnp.exp(-(gap[:, None, None] * rows) * rates[None])
    weight = jnp.where((earlier < position)[:, None, None], weight, 0.0)
    return jnp.sum(weight * every, axis=0)


def block_terms(values, rates, residues):
    length, width = values.shape
    blocks = length // BLOCK
    where_in = jnp.arange(BLOCK, dtype=jnp.float32)
    decay_in = jnp.exp(-where_in[:, None, None] * rates[None])
    impulse = jnp.sum(residues[None] * decay_in, axis=2)
    ii = lax.broadcasted_iota(jnp.int32, (BLOCK, BLOCK, BLOCK), 0)
    jj = lax.broadcasted_iota(jnp.int32, (BLOCK, BLOCK, BLOCK), 1)
    ll = lax.broadcasted_iota(jnp.int32, (BLOCK, BLOCK, BLOCK), 2)
    pick = (ii - jj == ll).astype(jnp.float32).reshape(BLOCK * BLOCK, BLOCK)
    toeplitz = jnp.dot(pick, impulse, precision=lax.Precision.HIGHEST).reshape(BLOCK, BLOCK, width)
    tails = decay_in[::-1]
    heads = residues[None] * decay_in * jnp.exp(-rates)[None]
    shaped = values.reshape(blocks, BLOCK, width)
    inner = jnp.einsum("ijc,bjc->bic", toeplitz, shaped, precision=lax.Precision.HIGHEST)
    ends = jnp.einsum("jcm,bjc->bcm", tails, shaped, precision=lax.Precision.HIGHEST)
    factor = jnp.broadcast_to(jnp.exp(-BLOCK * rates)[None], ends.shape)
    states, _ = lax.associative_scan(link_states, (ends, factor))
    starts = jnp.concatenate([jnp.zeros_like(states[:1]), states[:-1]], axis=0)
    offsets = jnp.exp(-(BLOCK * jnp.arange(blocks, dtype=jnp.float32))[:, None, None] * rates[None])
    return (inner, starts, states[-1], heads, offsets)


def link_states(earlier, later):
    return (later[0] + later[1] * earlier[0], earlier[1] * later[1])


def finish(inner, starts, heads, values, skip):
    carried = jnp.einsum("icm,bcm->bic", heads, starts, precision=lax.Precision.HIGHEST)
    return (inner + carried).reshape(values.shape) + skip[None] * values


def gathered_tokens(tokens, lanes):
    copies = jnp.broadcast_to(tokens[:, None], (tokens.shape[0], lanes, tokens.shape[1]))
    return lax.all_to_all(copies, CH, 1, 1)


def scattered_terms(terms, lanes):
    rows, total = terms.shape
    split = terms.reshape(rows, lanes, total // lanes)
    parts = lax.all_to_all(split, CH, 1, 1)
    return jnp.sum(parts.astype(jnp.float32), axis=1).astype(jnp.bfloat16)


def make_shards(count, lanes):
    def shards(tokens, in_weight, short_taps, rates, residues, skip, out_weight):
        rows = tokens.shape[0]
        width = in_weight.shape[2]
        whole = gathered_tokens(tokens, lanes)
        halo = passed_along(whole[rows - (SHORT - 1) :], CTX, count, 1)

        def across_yh(part):
            return lax.all_gather(part, "yh", axis=1)

        def across_z(part):
            part = lax.all_gather(part, "z", axis=2)
            return part.reshape(part.shape[0], -1, part.shape[-1])

        def shortened(weight):
            weight = weight.reshape(weight.shape[0], lanes, -1, weight.shape[-1])
            proj = jnp.einsum("tkd,jkdc->jtc", whole, weight, preferred_element_type=jnp.float32)
            earlier = jnp.einsum("tkd,jkdc->jtc", halo, weight, preferred_element_type=jnp.float32)
            proj = jnp.concatenate([earlier, proj], axis=1).astype(jnp.bfloat16)
            return proj.astype(jnp.float32)

        def filtered(widened, taps):
            feats = jnp.zeros((widened.shape[0], rows, width), jnp.float32)
            for i in range(SHORT):
                feats = feats + taps[i][:, None, :] * widened[:, SHORT - 1 - i : SHORT - 1 - i + rows, :]
            return feats

        pair = across_z(across_yh(in_weight[1:]))
        packed = jnp.concatenate([in_weight[0], out_weight.T], axis=1)[None]
        packed, pair = lax.optimization_barrier((packed, pair))
        feats = filtered(shortened(pair), short_taps[:, 1:])
        packed = across_z(across_yh(packed))[0]
        query = filtered(shortened(packed[None, :, :width]), short_taps[:, :1])[0]
        gated = (feats[0] * feats[1]).astype(jnp.bfloat16)
        values = gated.astype(jnp.float32)
        inner, starts, final, heads, offsets = block_terms(values, rates, residues)
        incoming = carried_in(final, rates, rows, count)
        starts = starts + offsets * incoming[None]
        conv = finish(inner, starts, heads, values, skip)
        hidden = (query * conv).astype(jnp.bfloat16)
        terms = jnp.einsum("tc,ec->te", hidden, packed[:, width:], preferred_element_type=jnp.float32)
        return scattered_terms(terms.astype(jnp.bfloat16), lanes)

    return shards


def solution(mesh):
    count = mesh.shape["ctx"]
    lanes = mesh.shape["ch"]
    fine = Mesh(mesh.devices.reshape(2, count // 2, lanes), CTX + (CH,))
    placed = (
        P(CTX, CH),
        P(None, CTX, CH),
        P(None, None, CH),
        P(CH, None),
        P(CH, None),
        P(CH),
        P(CH, CTX),
    )
    return jax.shard_map(
        make_shards(count, lanes), mesh=fine, in_specs=placed, out_specs=P(CTX, CH), check_vma=False
    )
```

```python
import jax
import jax.numpy as jnp
import numpy as np
from jax import lax
from jax.sharding import Mesh
from jax.sharding import PartitionSpec as P

SHORT = 3
BLOCK = 64
CTX = ("yh", "z")
CH = "ch"


def passed_along(block, axis, count, distance):
    route = [(i - distance, i) for i in range(count) if i - distance >= 0]
    return lax.ppermute(block, axis, route)


def carried_in(final, rates, rows, count):
    copies = jnp.broadcast_to(final[None], (count,) + final.shape)
    every = lax.all_to_all(copies, CTX, 0, 0)
    position = lax.axis_index(CTX)
    earlier = jnp.arange(count)
    gap = jnp.maximum(position - 1 - earlier, 0).astype(jnp.float32)
    weight = jnp.exp(-(gap[:, None, None] * rows) * rates[None])
    weight = jnp.where((earlier < position)[:, None, None], weight, 0.0)
    return jnp.sum(weight * every, axis=0)


def block_terms(values, rates, residues):
    length, width = values.shape
    blocks = length // BLOCK
    where_in = jnp.arange(BLOCK, dtype=jnp.float32)
    decay_in = jnp.exp(-where_in[:, None, None] * rates[None])
    impulse = jnp.sum(residues[None] * decay_in, axis=2)
    ii = lax.broadcasted_iota(jnp.int32, (BLOCK, BLOCK, BLOCK), 0)
    jj = lax.broadcasted_iota(jnp.int32, (BLOCK, BLOCK, BLOCK), 1)
    ll = lax.broadcasted_iota(jnp.int32, (BLOCK, BLOCK, BLOCK), 2)
    pick = (ii - jj == ll).astype(jnp.float32).reshape(BLOCK * BLOCK, BLOCK)
    toeplitz = jnp.dot(pick, impulse, precision=lax.Precision.HIGHEST).reshape(BLOCK, BLOCK, width)
    tails = decay_in[::-1]
    heads = residues[None] * decay_in * jnp.exp(-rates)[None]
    shaped = values.reshape(blocks, BLOCK, width)
    inner = jnp.einsum("ijc,bjc->bic", toeplitz, shaped, precision=lax.Precision.HIGHEST)
    ends = jnp.einsum("jcm,bjc->bcm", tails, shaped, precision=lax.Precision.HIGHEST)
    factor = jnp.broadcast_to(jnp.exp(-BLOCK * rates)[None], ends.shape)
    states, _ = lax.associative_scan(link_states, (ends, factor))
    starts = jnp.concatenate([jnp.zeros_like(states[:1]), states[:-1]], axis=0)
    offsets = jnp.exp(-(BLOCK * jnp.arange(blocks, dtype=jnp.float32))[:, None, None] * rates[None])
    return (inner, starts, states[-1], heads, offsets)


def link_states(earlier, later):
    return (later[0] + later[1] * earlier[0], earlier[1] * later[1])


def finish(inner, starts, heads, values, skip):
    carried = jnp.einsum("icm,bcm->bic", heads, starts, precision=lax.Precision.HIGHEST)
    return (inner + carried).reshape(values.shape) + skip[None] * values


def ring_z(block, zcount):
    ahead_route = [(i, (i + 1) % zcount) for i in range(zcount)]
    behind_route = [((i + 1) % zcount, i) for i in range(zcount)]
    ahead, behind = block, block
    got_ahead, got_behind = [], []
    for step in range(1, zcount // 2 + 1):
        ahead = lax.ppermute(ahead, "z", ahead_route)
        got_ahead.append(ahead)
        if step < zcount - step:
            behind = lax.ppermute(behind, "z", behind_route)
            got_behind.append(behind)
    by_offset = jnp.stack([block] + got_ahead + got_behind[::-1])
    flipped = by_offset[::-1]
    doubled = jnp.concatenate([flipped, flipped], axis=0)
    start = zcount - 1 - lax.axis_index("z")
    return lax.dynamic_slice_in_dim(doubled, start, zcount, axis=0)


def gathered_tokens(tokens, lanes):
    copies = jnp.broadcast_to(tokens[:, None], (tokens.shape[0], lanes, tokens.shape[1]))
    return lax.all_to_all(copies, CH, 1, 1)


def scattered_terms(terms, lanes):
    rows, total = terms.shape
    split = terms.reshape(rows, lanes, total // lanes)
    parts = lax.all_to_all(split, CH, 1, 1)
    return jnp.sum(parts.astype(jnp.float32), axis=1).astype(jnp.bfloat16)


def make_shards(count, lanes):
    def shards(tokens, in_weight, short_taps, rates, residues, skip, out_weight):
        rows = tokens.shape[0]
        width = in_weight.shape[2]
        whole = gathered_tokens(tokens, lanes)
        halo = passed_along(whole[rows - (SHORT - 1) :], CTX, count, 1)

        def across_yh(part):
            return lax.all_gather(part, "yh", axis=1)

        def across_z(part):
            part = lax.all_gather(part, "z", axis=2)
            return part.reshape(part.shape[0], -1, part.shape[-1])

        def shortened(weight):
            weight = weight.reshape(weight.shape[0], lanes, -1, weight.shape[-1])
            proj = jnp.einsum("tkd,jkdc->jtc", whole, weight, preferred_element_type=jnp.float32)
            earlier = jnp.einsum("tkd,jkdc->jtc", halo, weight, preferred_element_type=jnp.float32)
            proj = jnp.concatenate([earlier, proj], axis=1).astype(jnp.bfloat16)
            return proj.astype(jnp.float32)

        def filtered(widened, taps):
            feats = jnp.zeros((widened.shape[0], rows, width), jnp.float32)
            for i in range(SHORT):
                feats = feats + taps[i][:, None, :] * widened[:, SHORT - 1 - i : SHORT - 1 - i + rows, :]
            return feats

        packed = jnp.concatenate([in_weight[0], out_weight.T], axis=1)
        packed = lax.all_gather(packed, "yh", axis=0)
        packed = lax.all_gather(packed, "z", axis=1).reshape(-1, packed.shape[-1])
        pair = ring_z(across_yh(in_weight[1:]), count // 2)
        pair = jnp.transpose(pair, (1, 2, 0, 3, 4)).reshape(2, -1, width)
        feats = filtered(shortened(pair), short_taps[:, 1:])
        query = filtered(shortened(packed[None, :, :width]), short_taps[:, :1])[0]
        gated = (feats[0] * feats[1]).astype(jnp.bfloat16)
        values = gated.astype(jnp.float32)
        inner, starts, final, heads, offsets = block_terms(values, rates, residues)
        incoming = carried_in(final, rates, rows, count)
        starts = starts + offsets * incoming[None]
        conv = finish(inner, starts, heads, values, skip)
        hidden = (query * conv).astype(jnp.bfloat16)
        terms = jnp.einsum("tc,ec->te", hidden, packed[:, width:], preferred_element_type=jnp.float32)
        return scattered_terms(terms.astype(jnp.bfloat16), lanes)

    return shards


def solution(mesh):
    count = mesh.shape["ctx"]
    lanes = mesh.shape["ch"]
    fine = Mesh(mesh.devices.reshape(2, count // 2, lanes), CTX + (CH,))
    placed = (
        P(CTX, CH),
        P(None, CTX, CH),
        P(None, None, CH),
        P(CH, None),
        P(CH, None),
        P(CH),
        P(CH, CTX),
    )
    return jax.shard_map(
        make_shards(count, lanes), mesh=fine, in_specs=placed, out_specs=P(CTX, CH), check_vma=False
    )
```

```python
import jax
import jax.numpy as jnp
import numpy as np
from jax import lax
from jax.sharding import Mesh
from jax.sharding import PartitionSpec as P

SHORT = 3
BLOCK = 64
CTX = ("yh", "z")
CH = "ch"


def passed_along(block, axis, count, distance):
    route = [(i - distance, i) for i in range(count) if i - distance >= 0]
    return lax.ppermute(block, axis, route)


def carried_in(final, rates, rows, count):
    copies = jnp.broadcast_to(final[None], (count,) + final.shape)
    every = lax.all_to_all(copies, CTX, 0, 0)
    position = lax.axis_index(CTX)
    earlier = jnp.arange(count)
    gap = jnp.maximum(position - 1 - earlier, 0).astype(jnp.float32)
    weight = jnp.exp(-(gap[:, None, None] * rows) * rates[None])
    weight = jnp.where((earlier < position)[:, None, None], weight, 0.0)
    return jnp.sum(weight * every, axis=0)


def block_terms(values, rates, residues):
    length, width = values.shape
    blocks = length // BLOCK
    where_in = jnp.arange(BLOCK, dtype=jnp.float32)
    decay_in = jnp.exp(-where_in[:, None, None] * rates[None])
    impulse = jnp.sum(residues[None] * decay_in, axis=2)
    ii = lax.broadcasted_iota(jnp.int32, (BLOCK, BLOCK, BLOCK), 0)
    jj = lax.broadcasted_iota(jnp.int32, (BLOCK, BLOCK, BLOCK), 1)
    ll = lax.broadcasted_iota(jnp.int32, (BLOCK, BLOCK, BLOCK), 2)
    pick = (ii - jj == ll).astype(jnp.float32).reshape(BLOCK * BLOCK, BLOCK)
    toeplitz = jnp.dot(pick, impulse, precision=lax.Precision.HIGHEST).reshape(BLOCK, BLOCK, width)
    tails = decay_in[::-1]
    heads = residues[None] * decay_in * jnp.exp(-rates)[None]
    shaped = values.reshape(blocks, BLOCK, width)
    inner = jnp.einsum("ijc,bjc->bic", toeplitz, shaped, precision=lax.Precision.HIGHEST)
    ends = jnp.einsum("jcm,bjc->bcm", tails, shaped, precision=lax.Precision.HIGHEST)
    factor = jnp.broadcast_to(jnp.exp(-BLOCK * rates)[None], ends.shape)
    states, _ = lax.associative_scan(link_states, (ends, factor))
    starts = jnp.concatenate([jnp.zeros_like(states[:1]), states[:-1]], axis=0)
    offsets = jnp.exp(-(BLOCK * jnp.arange(blocks, dtype=jnp.float32))[:, None, None] * rates[None])
    return (inner, starts, states[-1], heads, offsets)


def link_states(earlier, later):
    return (later[0] + later[1] * earlier[0], earlier[1] * later[1])


def finish(inner, starts, heads, values, skip):
    carried = jnp.einsum("icm,bcm->bic", heads, starts, precision=lax.Precision.HIGHEST)
    return (inner + carried).reshape(values.shape) + skip[None] * values


def gathered_tokens(tokens, lanes):
    copies = jnp.broadcast_to(tokens[:, None], (tokens.shape[0], lanes, tokens.shape[1]))
    return lax.all_to_all(copies, CH, 1, 1)


def scattered_terms(terms, lanes):
    rows, total = terms.shape
    split = terms.reshape(rows, lanes, total // lanes)
    parts = lax.all_to_all(split, CH, 1, 1)
    return jnp.sum(parts.astype(jnp.float32), axis=1).astype(jnp.bfloat16)


def make_shards(count, lanes):
    def shards(tokens, in_weight, short_taps, rates, residues, skip, out_weight):
        rows = tokens.shape[0]
        width = in_weight.shape[2]
        whole = gathered_tokens(tokens, lanes)
        halo = passed_along(whole[rows - (SHORT - 1) :], CTX, count, 1)

        def across_yh(part):
            return lax.all_gather(part, "yh", axis=1)

        def across_z(part):
            part = lax.all_gather(part, "z", axis=2)
            return part.reshape(part.shape[0], -1, part.shape[-1])

        def shortened(weight):
            weight = weight.reshape(weight.shape[0], lanes, -1, weight.shape[-1])
            proj = jnp.einsum("tkd,jkdc->jtc", whole, weight, preferred_element_type=jnp.float32)
            earlier = jnp.einsum("tkd,jkdc->jtc", halo, weight, preferred_element_type=jnp.float32)
            proj = jnp.concatenate([earlier, proj], axis=1).astype(jnp.bfloat16)
            return proj.astype(jnp.float32)

        def filtered(widened, taps):
            feats = jnp.zeros((widened.shape[0], rows, width), jnp.float32)
            for i in range(SHORT):
                feats = feats + taps[i][:, None, :] * widened[:, SHORT - 1 - i : SHORT - 1 - i + rows, :]
            return feats

        pair = across_z(across_yh(in_weight[1:]))
        packed = jnp.stack([in_weight[0], out_weight.T])
        packed, pair = lax.optimization_barrier((packed, pair))
        feats = filtered(shortened(pair), short_taps[:, 1:])
        packed = across_z(across_yh(packed))
        query = filtered(shortened(packed[:1]), short_taps[:, :1])[0]
        gated = (feats[0] * feats[1]).astype(jnp.bfloat16)
        values = gated.astype(jnp.float32)
        inner, starts, final, heads, offsets = block_terms(values, rates, residues)
        incoming = carried_in(final, rates, rows, count)
        starts = starts + offsets * incoming[None]
        conv = finish(inner, starts, heads, values, skip)
        hidden = (query * conv).astype(jnp.bfloat16)
        terms = jnp.einsum("tc,ec->te", hidden, packed[1], preferred_element_type=jnp.float32)
        return scattered_terms(terms.astype(jnp.bfloat16), lanes)

    return shards


def solution(mesh):
    count = mesh.shape["ctx"]
    lanes = mesh.shape["ch"]
    fine = Mesh(mesh.devices.reshape(2, count // 2, lanes), CTX + (CH,))
    placed = (
        P(CTX, CH),
        P(None, CTX, CH),
        P(None, None, CH),
        P(CH, None),
        P(CH, None),
        P(CH),
        P(CH, CTX),
    )
    return jax.shard_map(
        make_shards(count, lanes), mesh=fine, in_specs=placed, out_specs=P(CTX, CH), check_vma=False
    )
```

```python
import jax
import jax.numpy as jnp
import numpy as np
from jax import lax
from jax.sharding import Mesh
from jax.sharding import PartitionSpec as P

SHORT = 3
BLOCK = 64
CTX = ("yh", "z")
CH = ("cx", "core")


def passed_along(block, axis, count, distance):
    route = [(i - distance, i) for i in range(count) if i - distance >= 0]
    return lax.ppermute(block, axis, route)


def carried_in(final, rates, rows, count):
    copies = jnp.broadcast_to(final[None], (count,) + final.shape)
    every = lax.all_to_all(copies, CTX, 0, 0)
    position = lax.axis_index(CTX)
    earlier = jnp.arange(count)
    gap = jnp.maximum(position - 1 - earlier, 0).astype(jnp.float32)
    weight = jnp.exp(-(gap[:, None, None] * rows) * rates[None])
    weight = jnp.where((earlier < position)[:, None, None], weight, 0.0)
    return jnp.sum(weight * every, axis=0)


def block_terms(values, rates, residues):
    length, width = values.shape
    blocks = length // BLOCK
    where_in = jnp.arange(BLOCK, dtype=jnp.float32)
    decay_in = jnp.exp(-where_in[:, None, None] * rates[None])
    impulse = jnp.sum(residues[None] * decay_in, axis=2)
    ii = lax.broadcasted_iota(jnp.int32, (BLOCK, BLOCK, BLOCK), 0)
    jj = lax.broadcasted_iota(jnp.int32, (BLOCK, BLOCK, BLOCK), 1)
    ll = lax.broadcasted_iota(jnp.int32, (BLOCK, BLOCK, BLOCK), 2)
    pick = (ii - jj == ll).astype(jnp.float32).reshape(BLOCK * BLOCK, BLOCK)
    toeplitz = jnp.dot(pick, impulse, precision=lax.Precision.HIGHEST).reshape(BLOCK, BLOCK, width)
    tails = decay_in[::-1]
    heads = residues[None] * decay_in * jnp.exp(-rates)[None]
    shaped = values.reshape(blocks, BLOCK, width)
    inner = jnp.einsum("ijc,bjc->bic", toeplitz, shaped, precision=lax.Precision.HIGHEST)
    ends = jnp.einsum("jcm,bjc->bcm", tails, shaped, precision=lax.Precision.HIGHEST)
    factor = jnp.broadcast_to(jnp.exp(-BLOCK * rates)[None], ends.shape)
    states, _ = lax.associative_scan(link_states, (ends, factor))
    starts = jnp.concatenate([jnp.zeros_like(states[:1]), states[:-1]], axis=0)
    offsets = jnp.exp(-(BLOCK * jnp.arange(blocks, dtype=jnp.float32))[:, None, None] * rates[None])
    return (inner, starts, states[-1], heads, offsets)


def link_states(earlier, later):
    return (later[0] + later[1] * earlier[0], earlier[1] * later[1])


def finish(inner, starts, heads, values, skip):
    carried = jnp.einsum("icm,bcm->bic", heads, starts, precision=lax.Precision.HIGHEST)
    return (inner + carried).reshape(values.shape) + skip[None] * values


def gathered_tokens(tokens, lanes):
    copies = jnp.broadcast_to(tokens[:, None], (tokens.shape[0], lanes, tokens.shape[1]))
    return lax.all_to_all(copies, CH, 1, 1)


def scattered_terms(terms, lanes):
    rows, total = terms.shape
    split = terms.reshape(rows, lanes // 2, 2, total // lanes)
    pairs = lax.all_to_all(split, "core", 2, 2)
    pairs = jnp.sum(pairs.astype(jnp.float32), axis=2).astype(jnp.bfloat16)
    parts = lax.all_to_all(pairs, "cx", 1, 1)
    return jnp.sum(parts.astype(jnp.float32), axis=1).astype(jnp.bfloat16)


def make_shards(count, lanes):
    def shards(tokens, in_weight, short_taps, rates, residues, skip, out_weight):
        rows = tokens.shape[0]
        width = in_weight.shape[2]
        whole = gathered_tokens(tokens, lanes)
        halo = passed_along(whole[rows - (SHORT - 1) :], CTX, count, 1)

        def across_yh(part):
            return lax.all_gather(part, "yh", axis=1)

        def across_z(part):
            part = lax.all_gather(part, "z", axis=2)
            return part.reshape(part.shape[0], -1, part.shape[-1])

        def shortened(weight):
            weight = weight.reshape(weight.shape[0], lanes, -1, weight.shape[-1])
            proj = jnp.einsum("tkd,jkdc->jtc", whole, weight, preferred_element_type=jnp.float32)
            earlier = jnp.einsum("tkd,jkdc->jtc", halo, weight, preferred_element_type=jnp.float32)
            proj = jnp.concatenate([earlier, proj], axis=1).astype(jnp.bfloat16)
            return proj.astype(jnp.float32)

        def filtered(widened, taps):
            feats = jnp.zeros((widened.shape[0], rows, width), jnp.float32)
            for i in range(SHORT):
                feats = feats + taps[i][:, None, :] * widened[:, SHORT - 1 - i : SHORT - 1 - i + rows, :]
            return feats

        pair = across_z(across_yh(in_weight[1:]))
        packed = jnp.concatenate([in_weight[0], out_weight.T], axis=1)[None]
        packed, pair = lax.optimization_barrier((packed, pair))
        feats = filtered(shortened(pair), short_taps[:, 1:])
        packed = across_z(across_yh(packed))[0]
        query = filtered(shortened(packed[None, :, :width]), short_taps[:, :1])[0]
        gated = (feats[0] * feats[1]).astype(jnp.bfloat16)
        values = gated.astype(jnp.float32)
        inner, starts, final, heads, offsets = block_terms(values, rates, residues)
        incoming = carried_in(final, rates, rows, count)
        starts = starts + offsets * incoming[None]
        conv = finish(inner, starts, heads, values, skip)
        hidden = (query * conv).astype(jnp.bfloat16)
        terms = jnp.einsum("tc,ec->te", hidden, packed[:, width:], preferred_element_type=jnp.float32)
        return scattered_terms(terms.astype(jnp.bfloat16), lanes)

    return shards


def solution(mesh):
    count = mesh.shape["ctx"]
    lanes = mesh.shape["ch"]
    fine = Mesh(mesh.devices.reshape(2, count // 2, lanes // 2, 2), CTX + CH)
    placed = (
        P(CTX, CH),
        P(None, CTX, CH),
        P(None, None, CH),
        P(CH, None),
        P(CH, None),
        P(CH),
        P(CH, CTX),
    )
    return jax.shard_map(
        make_shards(count, lanes), mesh=fine, in_specs=placed, out_specs=P(CTX, CH), check_vma=False
    )
```

```python
import jax
import jax.numpy as jnp
import numpy as np
from jax import lax
from jax.sharding import Mesh
from jax.sharding import PartitionSpec as P

SHORT = 3
BLOCK = 64
CTX = ("yh", "z")
CH = ("cx", "core")


def passed_along(block, axis, count, distance):
    route = [(i - distance, i) for i in range(count) if i - distance >= 0]
    return lax.ppermute(block, axis, route)


def carried_in(final, rates, rows, count):
    copies = jnp.broadcast_to(final[None], (count,) + final.shape)
    every = lax.all_to_all(copies, CTX, 0, 0)
    position = lax.axis_index(CTX)
    earlier = jnp.arange(count)
    gap = jnp.maximum(position - 1 - earlier, 0).astype(jnp.float32)
    weight = jnp.exp(-(gap[:, None, None] * rows) * rates[None])
    weight = jnp.where((earlier < position)[:, None, None], weight, 0.0)
    return jnp.sum(weight * every, axis=0)


def block_terms(values, rates, residues):
    length, width = values.shape
    blocks = length // BLOCK
    where_in = jnp.arange(BLOCK, dtype=jnp.float32)
    decay_in = jnp.exp(-where_in[:, None, None] * rates[None])
    impulse = jnp.sum(residues[None] * decay_in, axis=2)
    ii = lax.broadcasted_iota(jnp.int32, (BLOCK, BLOCK, BLOCK), 0)
    jj = lax.broadcasted_iota(jnp.int32, (BLOCK, BLOCK, BLOCK), 1)
    ll = lax.broadcasted_iota(jnp.int32, (BLOCK, BLOCK, BLOCK), 2)
    pick = (ii - jj == ll).astype(jnp.float32).reshape(BLOCK * BLOCK, BLOCK)
    toeplitz = jnp.dot(pick, impulse, precision=lax.Precision.HIGHEST).reshape(BLOCK, BLOCK, width)
    tails = decay_in[::-1]
    heads = residues[None] * decay_in * jnp.exp(-rates)[None]
    shaped = values.reshape(blocks, BLOCK, width)
    inner = jnp.einsum("ijc,bjc->bic", toeplitz, shaped, precision=lax.Precision.HIGHEST)
    ends = jnp.einsum("jcm,bjc->bcm", tails, shaped, precision=lax.Precision.HIGHEST)
    factor = jnp.broadcast_to(jnp.exp(-BLOCK * rates)[None], ends.shape)
    states, _ = lax.associative_scan(link_states, (ends, factor))
    starts = jnp.concatenate([jnp.zeros_like(states[:1]), states[:-1]], axis=0)
    offsets = jnp.exp(-(BLOCK * jnp.arange(blocks, dtype=jnp.float32))[:, None, None] * rates[None])
    return (inner, starts, states[-1], heads, offsets)


def link_states(earlier, later):
    return (later[0] + later[1] * earlier[0], earlier[1] * later[1])


def finish(inner, starts, heads, values, skip):
    carried = jnp.einsum("icm,bcm->bic", heads, starts, precision=lax.Precision.HIGHEST)
    return (inner + carried).reshape(values.shape) + skip[None] * values


def gathered_tokens(tokens, lanes):
    copies = jnp.broadcast_to(tokens[:, None], (tokens.shape[0], lanes, tokens.shape[1]))
    return lax.all_to_all(copies, CH, 1, 1)


def scattered_terms(terms):
    pairs = lax.all_to_all(terms, "core", 0, 0)
    pairs = jnp.sum(pairs.astype(jnp.float32), axis=0).astype(jnp.bfloat16)
    parts = lax.all_to_all(pairs, "cx", 0, 0)
    return jnp.sum(parts.astype(jnp.float32), axis=0).astype(jnp.bfloat16)


def make_shards(count, lanes):
    def shards(tokens, in_weight, short_taps, rates, residues, skip, out_weight):
        rows = tokens.shape[0]
        width = in_weight.shape[2]
        whole = gathered_tokens(tokens, lanes)
        halo = passed_along(whole[rows - (SHORT - 1) :], CTX, count, 1)

        def across_yh(part):
            return lax.all_gather(part, "yh", axis=1)

        def across_z(part):
            part = lax.all_gather(part, "z", axis=2)
            return part.reshape(part.shape[0], -1, part.shape[-1])

        def shortened(weight):
            weight = weight.reshape(weight.shape[0], lanes, -1, weight.shape[-1])
            proj = jnp.einsum("tkd,jkdc->jtc", whole, weight, preferred_element_type=jnp.float32)
            earlier = jnp.einsum("tkd,jkdc->jtc", halo, weight, preferred_element_type=jnp.float32)
            proj = jnp.concatenate([earlier, proj], axis=1).astype(jnp.bfloat16)
            return proj.astype(jnp.float32)

        def filtered(widened, taps):
            feats = jnp.zeros((widened.shape[0], rows, width), jnp.float32)
            for i in range(SHORT):
                feats = feats + taps[i][:, None, :] * widened[:, SHORT - 1 - i : SHORT - 1 - i + rows, :]
            return feats

        pair = across_z(across_yh(in_weight[1:]))
        packed = jnp.concatenate([in_weight[0], out_weight.T], axis=1)[None]
        packed, pair = lax.optimization_barrier((packed, pair))
        feats = filtered(shortened(pair), short_taps[:, 1:])
        packed = across_z(across_yh(packed))[0]
        query = filtered(shortened(packed[None, :, :width]), short_taps[:, :1])[0]
        gated = (feats[0] * feats[1]).astype(jnp.bfloat16)
        values = gated.astype(jnp.float32)
        inner, starts, final, heads, offsets = block_terms(values, rates, residues)
        incoming = carried_in(final, rates, rows, count)
        starts = starts + offsets * incoming[None]
        conv = finish(inner, starts, heads, values, skip)
        hidden = (query * conv).astype(jnp.bfloat16)
        out_w = jnp.transpose(packed[:, width:].reshape(lanes // 2, 2, -1, width), (1, 0, 2, 3))
        terms = jnp.einsum("tc,yxec->yxte", hidden, out_w, preferred_element_type=jnp.float32)
        return scattered_terms(terms.astype(jnp.bfloat16))

    return shards


def solution(mesh):
    count = mesh.shape["ctx"]
    lanes = mesh.shape["ch"]
    fine = Mesh(mesh.devices.reshape(2, count // 2, lanes // 2, 2), CTX + CH)
    placed = (
        P(CTX, CH),
        P(None, CTX, CH),
        P(None, None, CH),
        P(CH, None),
        P(CH, None),
        P(CH),
        P(CH, CTX),
    )
    return jax.shard_map(
        make_shards(count, lanes), mesh=fine, in_specs=placed, out_specs=P(CTX, CH), check_vma=False
    )
```

```python
import jax
import jax.numpy as jnp
import numpy as np
from jax import lax
from jax.sharding import Mesh
from jax.sharding import PartitionSpec as P

SHORT = 3
BLOCK = 64
CTX = ("yh", "z")
CH = ("cx", "core")


def passed_along(block, axis, count, distance):
    route = [(i - distance, i) for i in range(count) if i - distance >= 0]
    return lax.ppermute(block, axis, route)


def carried_in(final, rates, rows, count):
    copies = jnp.broadcast_to(final[None], (count,) + final.shape)
    every = lax.all_to_all(copies, CTX, 0, 0)
    position = lax.axis_index(CTX)
    earlier = jnp.arange(count)
    gap = jnp.maximum(position - 1 - earlier, 0).astype(jnp.float32)
    weight = jnp.exp(-(gap[:, None, None] * rows) * rates[None])
    weight = jnp.where((earlier < position)[:, None, None], weight, 0.0)
    return jnp.sum(weight * every, axis=0)


def block_terms(values, rates, residues):
    length, width = values.shape
    blocks = length // BLOCK
    where_in = jnp.arange(BLOCK, dtype=jnp.float32)
    decay_in = jnp.exp(-where_in[:, None, None] * rates[None])
    impulse = jnp.sum(residues[None] * decay_in, axis=2)
    ii = lax.broadcasted_iota(jnp.int32, (BLOCK, BLOCK, BLOCK), 0)
    jj = lax.broadcasted_iota(jnp.int32, (BLOCK, BLOCK, BLOCK), 1)
    ll = lax.broadcasted_iota(jnp.int32, (BLOCK, BLOCK, BLOCK), 2)
    pick = (ii - jj == ll).astype(jnp.float32).reshape(BLOCK * BLOCK, BLOCK)
    toeplitz = jnp.dot(pick, impulse, precision=lax.Precision.HIGHEST).reshape(BLOCK, BLOCK, width)
    tails = decay_in[::-1]
    heads = residues[None] * decay_in * jnp.exp(-rates)[None]
    shaped = values.reshape(blocks, BLOCK, width)
    inner = jnp.einsum("ijc,bjc->bic", toeplitz, shaped, precision=lax.Precision.HIGHEST)
    ends = jnp.einsum("jcm,bjc->bcm", tails, shaped, precision=lax.Precision.HIGHEST)
    factor = jnp.broadcast_to(jnp.exp(-BLOCK * rates)[None], ends.shape)
    states, _ = lax.associative_scan(link_states, (ends, factor))
    starts = jnp.concatenate([jnp.zeros_like(states[:1]), states[:-1]], axis=0)
    offsets = jnp.exp(-(BLOCK * jnp.arange(blocks, dtype=jnp.float32))[:, None, None] * rates[None])
    return (inner, starts, states[-1], heads, offsets)


def link_states(earlier, later):
    return (later[0] + later[1] * earlier[0], earlier[1] * later[1])


def finish(inner, starts, heads, values, skip):
    carried = jnp.einsum("icm,bcm->bic", heads, starts, precision=lax.Precision.HIGHEST)
    return (inner + carried).reshape(values.shape) + skip[None] * values


def gathered_tokens(tokens, lanes):
    copies = jnp.broadcast_to(tokens[:, None], (tokens.shape[0], lanes, tokens.shape[1]))
    return lax.all_to_all(copies, CH, 1, 1)


def scattered_terms(terms):
    pairs = lax.all_to_all(terms, "core", 0, 0)
    pairs = jnp.sum(pairs.astype(jnp.float32), axis=0).astype(jnp.bfloat16)
    parts = lax.all_to_all(pairs, "cx", 0, 0)
    return jnp.sum(parts.astype(jnp.float32), axis=0).astype(jnp.bfloat16)


def make_shards(count, lanes):
    def shards(tokens, in_weight, short_taps, rates, residues, skip, out_weight):
        rows = tokens.shape[0]
        width = in_weight.shape[2]
        whole = gathered_tokens(tokens, lanes)
        halo = passed_along(whole[rows - (SHORT - 1) :], CTX, count, 1)

        def across_yh(part):
            return lax.all_gather(part, "yh", axis=1)

        def across_z(part):
            part = lax.all_gather(part, "z", axis=2)
            return part.reshape(part.shape[0], -1, part.shape[-1])

        def shortened(weight):
            weight = weight.reshape(weight.shape[0], lanes, -1, weight.shape[-1])
            proj = jnp.einsum("tkd,jkdc->jtc", whole, weight, preferred_element_type=jnp.float32)
            earlier = jnp.einsum("tkd,jkdc->jtc", halo, weight, preferred_element_type=jnp.float32)
            proj = jnp.concatenate([earlier, proj], axis=1).astype(jnp.bfloat16)
            return proj.astype(jnp.float32)

        def filtered(widened, taps):
            feats = jnp.zeros((widened.shape[0], rows, width), jnp.float32)
            for i in range(SHORT):
                feats = feats + taps[i][:, None, :] * widened[:, SHORT - 1 - i : SHORT - 1 - i + rows, :]
            return feats

        streams = across_z(across_yh(in_weight))
        packed = out_weight.T[None]
        packed, streams = lax.optimization_barrier((packed, streams))
        feats = filtered(shortened(streams), short_taps)
        packed = across_z(across_yh(packed))[0]
        query = feats[0]
        feats = feats[1:]
        gated = (feats[0] * feats[1]).astype(jnp.bfloat16)
        values = gated.astype(jnp.float32)
        inner, starts, final, heads, offsets = block_terms(values, rates, residues)
        incoming = carried_in(final, rates, rows, count)
        starts = starts + offsets * incoming[None]
        conv = finish(inner, starts, heads, values, skip)
        hidden = (query * conv).astype(jnp.bfloat16)
        out_w = jnp.transpose(packed.reshape(lanes // 2, 2, -1, width), (1, 0, 2, 3))
        terms = jnp.einsum("tc,yxec->yxte", hidden, out_w, preferred_element_type=jnp.float32)
        return scattered_terms(terms.astype(jnp.bfloat16))

    return shards


def solution(mesh):
    count = mesh.shape["ctx"]
    lanes = mesh.shape["ch"]
    fine = Mesh(mesh.devices.reshape(2, count // 2, lanes // 2, 2), CTX + CH)
    placed = (
        P(CTX, CH),
        P(None, CTX, CH),
        P(None, None, CH),
        P(CH, None),
        P(CH, None),
        P(CH),
        P(CH, CTX),
    )
    return jax.shard_map(
        make_shards(count, lanes), mesh=fine, in_specs=placed, out_specs=P(CTX, CH), check_vma=False
    )
```

```python
import jax
import jax.numpy as jnp
import numpy as np
from jax import lax
from jax.sharding import Mesh
from jax.sharding import PartitionSpec as P

SHORT = 3
BLOCK = 64
CTX = ("yh", "z")
CH = ("cx", "core")


def passed_along(block, axis, count, distance):
    route = [(i - distance, i) for i in range(count) if i - distance >= 0]
    return lax.ppermute(block, axis, route)


def carried_in(final, rates, rows, count):
    copies = jnp.broadcast_to(final[None], (count,) + final.shape)
    every = lax.all_to_all(copies, CTX, 0, 0)
    position = lax.axis_index(CTX)
    earlier = jnp.arange(count)
    gap = jnp.maximum(position - 1 - earlier, 0).astype(jnp.float32)
    weight = jnp.exp(-(gap[:, None, None] * rows) * rates[None])
    weight = jnp.where((earlier < position)[:, None, None], weight, 0.0)
    return jnp.sum(weight * every, axis=0)


def block_terms(values, rates, residues):
    length, width = values.shape
    blocks = length // BLOCK
    where_in = jnp.arange(BLOCK, dtype=jnp.float32)
    decay_in = jnp.exp(-where_in[:, None, None] * rates[None])
    impulse = jnp.sum(residues[None] * decay_in, axis=2)
    ii = lax.broadcasted_iota(jnp.int32, (BLOCK, BLOCK, BLOCK), 0)
    jj = lax.broadcasted_iota(jnp.int32, (BLOCK, BLOCK, BLOCK), 1)
    ll = lax.broadcasted_iota(jnp.int32, (BLOCK, BLOCK, BLOCK), 2)
    pick = (ii - jj == ll).astype(jnp.float32).reshape(BLOCK * BLOCK, BLOCK)
    toeplitz = jnp.dot(pick, impulse, precision=lax.Precision.HIGHEST).reshape(BLOCK, BLOCK, width)
    tails = decay_in[::-1]
    heads = residues[None] * decay_in * jnp.exp(-rates)[None]
    shaped = values.reshape(blocks, BLOCK, width)
    inner = jnp.einsum("ijc,bjc->bic", toeplitz, shaped, precision=lax.Precision.HIGHEST)
    ends = jnp.einsum("jcm,bjc->bcm", tails, shaped, precision=lax.Precision.HIGHEST)
    factor = jnp.broadcast_to(jnp.exp(-BLOCK * rates)[None], ends.shape)
    states, _ = lax.associative_scan(link_states, (ends, factor))
    starts = jnp.concatenate([jnp.zeros_like(states[:1]), states[:-1]], axis=0)
    offsets = jnp.exp(-(BLOCK * jnp.arange(blocks, dtype=jnp.float32))[:, None, None] * rates[None])
    return (inner, starts, states[-1], heads, offsets)


def link_states(earlier, later):
    return (later[0] + later[1] * earlier[0], earlier[1] * later[1])


def finish(inner, starts, heads, values, skip):
    carried = jnp.einsum("icm,bcm->bic", heads, starts, precision=lax.Precision.HIGHEST)
    return (inner + carried).reshape(values.shape) + skip[None] * values


def gathered_tokens(tokens, lanes):
    copies = jnp.broadcast_to(tokens[:, None], (tokens.shape[0], lanes, tokens.shape[1]))
    return lax.all_to_all(copies, CH, 1, 1)


def scattered_terms(terms):
    pairs = lax.all_to_all(terms, "core", 0, 0)
    pairs = jnp.sum(pairs.astype(jnp.float32), axis=0).astype(jnp.bfloat16)
    parts = lax.all_to_all(pairs, "cx", 0, 0)
    return jnp.sum(parts.astype(jnp.float32), axis=0).astype(jnp.bfloat16)


def make_shards(count, lanes):
    def shards(tokens, in_weight, short_taps, rates, residues, skip, out_weight):
        rows = tokens.shape[0]
        width = in_weight.shape[2]
        whole = gathered_tokens(tokens, lanes)
        halo = passed_along(whole[rows - (SHORT - 1) :], CTX, count, 1)

        def across_yh(part):
            return lax.all_gather(part, "yh", axis=1)

        def across_z(part):
            part = lax.all_gather(part, "z", axis=2)
            return part.reshape(part.shape[0], -1, part.shape[-1])

        def shortened(weight):
            weight = weight.reshape(weight.shape[0], lanes, -1, weight.shape[-1])
            proj = jnp.einsum("tkd,jkdc->jtc", whole, weight, preferred_element_type=jnp.float32)
            earlier = jnp.einsum("tkd,jkdc->jtc", halo, weight, preferred_element_type=jnp.float32)
            proj = jnp.concatenate([earlier, proj], axis=1).astype(jnp.bfloat16)
            return proj.astype(jnp.float32)

        def filtered(widened, taps):
            feats = jnp.zeros((widened.shape[0], rows, width), jnp.float32)
            for i in range(SHORT):
                feats = feats + taps[i][:, None, :] * widened[:, SHORT - 1 - i : SHORT - 1 - i + rows, :]
            return feats

        streams = across_yh(in_weight)
        packed = lax.all_gather(out_weight, "yh", axis=1)
        packed, streams = lax.optimization_barrier((packed, streams))
        streams = across_z(streams)
        packed, streams = lax.optimization_barrier((packed, streams))
        feats = filtered(shortened(streams), short_taps)
        packed = lax.all_gather(packed, "z", axis=2).reshape(width, -1)
        query = feats[0]
        feats = feats[1:]
        gated = (feats[0] * feats[1]).astype(jnp.bfloat16)
        values = gated.astype(jnp.float32)
        inner, starts, final, heads, offsets = block_terms(values, rates, residues)
        incoming = carried_in(final, rates, rows, count)
        starts = starts + offsets * incoming[None]
        conv = finish(inner, starts, heads, values, skip)
        hidden = (query * conv).astype(jnp.bfloat16)
        out_w = jnp.transpose(packed.reshape(width, lanes // 2, 2, -1), (0, 2, 1, 3))
        terms = jnp.einsum("tc,cyxe->yxte", hidden, out_w, preferred_element_type=jnp.float32)
        return scattered_terms(terms.astype(jnp.bfloat16))

    return shards


def solution(mesh):
    count = mesh.shape["ctx"]
    lanes = mesh.shape["ch"]
    fine = Mesh(mesh.devices.reshape(2, count // 2, lanes // 2, 2), CTX + CH)
    placed = (
        P(CTX, CH),
        P(None, CTX, CH),
        P(None, None, CH),
        P(CH, None),
        P(CH, None),
        P(CH),
        P(CH, CTX),
    )
    return jax.shard_map(
        make_shards(count, lanes), mesh=fine, in_specs=placed, out_specs=P(CTX, CH), check_vma=False
    )
```

```python
import jax
import jax.numpy as jnp
import numpy as np
from jax import lax
from jax.sharding import Mesh
from jax.sharding import PartitionSpec as P

SHORT = 3
BLOCK = 64
CTX = ("yh", "z")
CH = ("cx", "core")


def passed_along(block, axis, count, distance):
    route = [(i - distance, i) for i in range(count) if i - distance >= 0]
    return lax.ppermute(block, axis, route)


def carried_in(final, rates, rows, count):
    copies = jnp.broadcast_to(final[None], (count,) + final.shape)
    every = lax.all_to_all(copies, CTX, 0, 0)
    position = lax.axis_index(CTX)
    earlier = jnp.arange(count)
    gap = jnp.maximum(position - 1 - earlier, 0).astype(jnp.float32)
    weight = jnp.exp(-(gap[:, None, None] * rows) * rates[None])
    weight = jnp.where((earlier < position)[:, None, None], weight, 0.0)
    return jnp.sum(weight * every, axis=0)


def block_terms(values, rates, residues):
    length, width = values.shape
    blocks = length // BLOCK
    where_in = jnp.arange(BLOCK, dtype=jnp.float32)
    decay_in = jnp.exp(-where_in[:, None, None] * rates[None])
    impulse = jnp.sum(residues[None] * decay_in, axis=2)
    ii = lax.broadcasted_iota(jnp.int32, (BLOCK, BLOCK, BLOCK), 0)
    jj = lax.broadcasted_iota(jnp.int32, (BLOCK, BLOCK, BLOCK), 1)
    ll = lax.broadcasted_iota(jnp.int32, (BLOCK, BLOCK, BLOCK), 2)
    pick = (ii - jj == ll).astype(jnp.float32).reshape(BLOCK * BLOCK, BLOCK)
    toeplitz = jnp.dot(pick, impulse, precision=lax.Precision.HIGHEST).reshape(BLOCK, BLOCK, width)
    tails = decay_in[::-1]
    heads = residues[None] * decay_in * jnp.exp(-rates)[None]
    shaped = values.reshape(blocks, BLOCK, width)
    inner = jnp.einsum("ijc,bjc->bic", toeplitz, shaped, precision=lax.Precision.HIGHEST)
    ends = jnp.einsum("jcm,bjc->bcm", tails, shaped, precision=lax.Precision.HIGHEST)
    factor = jnp.broadcast_to(jnp.exp(-BLOCK * rates)[None], ends.shape)
    states, _ = lax.associative_scan(link_states, (ends, factor))
    starts = jnp.concatenate([jnp.zeros_like(states[:1]), states[:-1]], axis=0)
    offsets = jnp.exp(-(BLOCK * jnp.arange(blocks, dtype=jnp.float32))[:, None, None] * rates[None])
    return (inner, starts, states[-1], heads, offsets)


def link_states(earlier, later):
    return (later[0] + later[1] * earlier[0], earlier[1] * later[1])


def finish(inner, starts, heads, values, skip):
    carried = jnp.einsum("icm,bcm->bic", heads, starts, precision=lax.Precision.HIGHEST)
    return (inner + carried).reshape(values.shape) + skip[None] * values


def gathered_tokens(tokens, lanes):
    copies = jnp.broadcast_to(tokens[:, None], (tokens.shape[0], lanes, tokens.shape[1]))
    return lax.all_to_all(copies, CH, 1, 1)


def scattered_terms(terms):
    pairs = lax.all_to_all(terms, "core", 0, 0)
    pairs = jnp.sum(pairs.astype(jnp.float32), axis=0).astype(jnp.bfloat16)
    parts = lax.all_to_all(pairs, "cx", 0, 0)
    return jnp.sum(parts.astype(jnp.float32), axis=0).astype(jnp.bfloat16)


def make_shards(count, lanes):
    def shards(tokens, in_weight, short_taps, rates, residues, skip, out_weight):
        rows = tokens.shape[0]
        width = in_weight.shape[2]
        whole = gathered_tokens(tokens, lanes)
        halo = passed_along(whole[rows - (SHORT - 1) :], CTX, count, 1)

        def across_yh(part):
            return lax.all_gather(part, "yh", axis=1)

        def across_z(part):
            part = lax.all_gather(part, "z", axis=2)
            return part.reshape(part.shape[0], -1, part.shape[-1])

        def shortened(weight):
            weight = weight.reshape(weight.shape[0], lanes, -1, weight.shape[-1])
            proj = jnp.einsum("tkd,jkdc->jtc", whole, weight, preferred_element_type=jnp.float32)
            earlier = jnp.einsum("tkd,jkdc->jtc", halo, weight, preferred_element_type=jnp.float32)
            proj = jnp.concatenate([earlier, proj], axis=1).astype(jnp.bfloat16)
            return proj.astype(jnp.float32)

        def filtered(widened, taps):
            feats = jnp.zeros((widened.shape[0], rows, width), jnp.float32)
            for i in range(SHORT):
                feats = feats + taps[i][:, None, :] * widened[:, SHORT - 1 - i : SHORT - 1 - i + rows, :]
            return feats

        streams = across_yh(in_weight)
        packed = lax.all_gather(out_weight, "yh", axis=1)
        packed, streams = lax.optimization_barrier((packed, streams))
        streams = across_z(streams)
        feats = filtered(shortened(streams), short_taps)
        packed = lax.all_gather(packed, "z", axis=2).reshape(width, -1)
        query = feats[0]
        feats = feats[1:]
        gated = (feats[0] * feats[1]).astype(jnp.bfloat16)
        values = gated.astype(jnp.float32)
        inner, starts, final, heads, offsets = block_terms(values, rates, residues)
        incoming = carried_in(final, rates, rows, count)
        starts = starts + offsets * incoming[None]
        conv = finish(inner, starts, heads, values, skip)
        hidden = (query * conv).astype(jnp.bfloat16)
        out_w = jnp.transpose(packed.reshape(width, lanes // 2, 2, -1), (0, 2, 1, 3))
        terms = jnp.einsum("tc,cyxe->yxte", hidden, out_w, preferred_element_type=jnp.float32)
        return scattered_terms(terms.astype(jnp.bfloat16))

    return shards


def solution(mesh):
    count = mesh.shape["ctx"]
    lanes = mesh.shape["ch"]
    fine = Mesh(mesh.devices.reshape(2, count // 2, lanes // 2, 2), CTX + CH)
    placed = (
        P(CTX, CH),
        P(None, CTX, CH),
        P(None, None, CH),
        P(CH, None),
        P(CH, None),
        P(CH),
        P(CH, CTX),
    )
    return jax.shard_map(
        make_shards(count, lanes), mesh=fine, in_specs=placed, out_specs=P(CTX, CH), check_vma=False
    )
```

```python
import jax
import jax.numpy as jnp
import numpy as np
from jax import lax
from jax.sharding import Mesh
from jax.sharding import PartitionSpec as P

SHORT = 3
BLOCK = 64
CTX = ("yh", "z")
CH = ("cx", "core")


def passed_along(block, axis, count, distance):
    route = [(i - distance, i) for i in range(count) if i - distance >= 0]
    return lax.ppermute(block, axis, route)


def carried_in(final, rates, rows, count):
    copies = jnp.broadcast_to(final[None], (count,) + final.shape)
    every = lax.all_to_all(copies, CTX, 0, 0)
    position = lax.axis_index(CTX)
    earlier = jnp.arange(count)
    gap = jnp.maximum(position - 1 - earlier, 0).astype(jnp.float32)
    weight = jnp.exp(-(gap[:, None, None] * rows) * rates[None])
    weight = jnp.where((earlier < position)[:, None, None], weight, 0.0)
    return jnp.sum(weight * every, axis=0)


def block_terms(values, rates, residues):
    length, width = values.shape
    blocks = length // BLOCK
    where_in = jnp.arange(BLOCK, dtype=jnp.float32)
    decay_in = jnp.exp(-where_in[:, None, None] * rates[None])
    impulse = jnp.sum(residues[None] * decay_in, axis=2)
    ii = lax.broadcasted_iota(jnp.int32, (BLOCK, BLOCK, BLOCK), 0)
    jj = lax.broadcasted_iota(jnp.int32, (BLOCK, BLOCK, BLOCK), 1)
    ll = lax.broadcasted_iota(jnp.int32, (BLOCK, BLOCK, BLOCK), 2)
    pick = (ii - jj == ll).astype(jnp.float32).reshape(BLOCK * BLOCK, BLOCK)
    toeplitz = jnp.dot(pick, impulse, precision=lax.Precision.HIGHEST).reshape(BLOCK, BLOCK, width)
    tails = decay_in[::-1]
    heads = residues[None] * decay_in * jnp.exp(-rates)[None]
    shaped = values.reshape(blocks, BLOCK, width)
    inner = jnp.einsum("ijc,bjc->bic", toeplitz, shaped, precision=lax.Precision.HIGHEST)
    ends = jnp.einsum("jcm,bjc->bcm", tails, shaped, precision=lax.Precision.HIGHEST)
    factor = jnp.broadcast_to(jnp.exp(-BLOCK * rates)[None], ends.shape)
    states, _ = lax.associative_scan(link_states, (ends, factor))
    starts = jnp.concatenate([jnp.zeros_like(states[:1]), states[:-1]], axis=0)
    offsets = jnp.exp(-(BLOCK * jnp.arange(blocks, dtype=jnp.float32))[:, None, None] * rates[None])
    return (inner, starts, states[-1], heads, offsets)


def link_states(earlier, later):
    return (later[0] + later[1] * earlier[0], earlier[1] * later[1])


def finish(inner, starts, heads, values, skip):
    carried = jnp.einsum("icm,bcm->bic", heads, starts, precision=lax.Precision.HIGHEST)
    return (inner + carried).reshape(values.shape) + skip[None] * values


def gathered_tokens(tokens, lanes):
    copies = jnp.broadcast_to(tokens[:, None], (tokens.shape[0], lanes, tokens.shape[1]))
    return lax.all_to_all(copies, CH, 1, 1)


def scattered_terms(terms):
    pairs = lax.all_to_all(terms, "core", 0, 0)
    pairs = jnp.sum(pairs.astype(jnp.float32), axis=0).astype(jnp.bfloat16)
    parts = lax.all_to_all(pairs, "cx", 0, 0)
    return jnp.sum(parts.astype(jnp.float32), axis=0).astype(jnp.bfloat16)


def make_shards(count, lanes):
    def shards(tokens, in_weight, short_taps, rates, residues, skip, out_weight):
        rows = tokens.shape[0]
        width = in_weight.shape[2]
        whole = gathered_tokens(tokens, lanes)
        halo = passed_along(whole[rows - (SHORT - 1) :], CTX, count, 1)

        def across_yh(part):
            return lax.all_gather(part, "yh", axis=1)

        def across_z(part):
            part = lax.all_gather(part, "z", axis=2)
            return part.reshape(part.shape[0], -1, part.shape[-1])

        def shortened(weight):
            weight = weight.reshape(weight.shape[0], lanes, -1, weight.shape[-1])
            proj = jnp.einsum("tkd,jkdc->jtc", whole, weight, preferred_element_type=jnp.float32)
            earlier = jnp.einsum("tkd,jkdc->jtc", halo, weight, preferred_element_type=jnp.float32)
            proj = jnp.concatenate([earlier, proj], axis=1).astype(jnp.bfloat16)
            return proj.astype(jnp.float32)

        def filtered(widened, taps):
            feats = jnp.zeros((widened.shape[0], rows, width), jnp.float32)
            for i in range(SHORT):
                feats = feats + taps[i][:, None, :] * widened[:, SHORT - 1 - i : SHORT - 1 - i + rows, :]
            return feats

        streams = across_yh(in_weight)
        packed, streams = lax.optimization_barrier((out_weight, streams))
        streams = across_z(streams)
        packed = lax.all_gather(packed, "yh", axis=1)
        feats = filtered(shortened(streams), short_taps)
        packed = lax.all_gather(packed, "z", axis=2).reshape(width, -1)
        query = feats[0]
        feats = feats[1:]
        gated = (feats[0] * feats[1]).astype(jnp.bfloat16)
        values = gated.astype(jnp.float32)
        inner, starts, final, heads, offsets = block_terms(values, rates, residues)
        incoming = carried_in(final, rates, rows, count)
        starts = starts + offsets * incoming[None]
        conv = finish(inner, starts, heads, values, skip)
        hidden = (query * conv).astype(jnp.bfloat16)
        out_w = jnp.transpose(packed.reshape(width, lanes // 2, 2, -1), (0, 2, 1, 3))
        terms = jnp.einsum("tc,cyxe->yxte", hidden, out_w, preferred_element_type=jnp.float32)
        return scattered_terms(terms.astype(jnp.bfloat16))

    return shards


def solution(mesh):
    count = mesh.shape["ctx"]
    lanes = mesh.shape["ch"]
    fine = Mesh(mesh.devices.reshape(2, count // 2, lanes // 2, 2), CTX + CH)
    placed = (
        P(CTX, CH),
        P(None, CTX, CH),
        P(None, None, CH),
        P(CH, None),
        P(CH, None),
        P(CH),
        P(CH, CTX),
    )
    return jax.shard_map(
        make_shards(count, lanes), mesh=fine, in_specs=placed, out_specs=P(CTX, CH), check_vma=False
    )
```

```python
import jax
import jax.numpy as jnp
import numpy as np
from jax import lax
from jax.sharding import Mesh
from jax.sharding import PartitionSpec as P

SHORT = 3
BLOCK = 64
CTX = ("yh", "z")
CH = ("cx", "core")


def passed_along(block, axis, count, distance):
    route = [(i - distance, i) for i in range(count) if i - distance >= 0]
    return lax.ppermute(block, axis, route)


def carried_in(final, rates, rows, count):
    copies = jnp.broadcast_to(final[None], (count,) + final.shape)
    every = lax.all_to_all(copies, CTX, 0, 0)
    position = lax.axis_index(CTX)
    earlier = jnp.arange(count)
    gap = jnp.maximum(position - 1 - earlier, 0).astype(jnp.float32)
    weight = jnp.exp(-(gap[:, None, None] * rows) * rates[None])
    weight = jnp.where((earlier < position)[:, None, None], weight, 0.0)
    return jnp.sum(weight * every, axis=0)


def block_terms(values, rates, residues):
    length, width = values.shape
    blocks = length // BLOCK
    where_in = jnp.arange(BLOCK, dtype=jnp.float32)
    decay_in = jnp.exp(-where_in[:, None, None] * rates[None])
    impulse = jnp.sum(residues[None] * decay_in, axis=2)
    ii = lax.broadcasted_iota(jnp.int32, (BLOCK, BLOCK, BLOCK), 0)
    jj = lax.broadcasted_iota(jnp.int32, (BLOCK, BLOCK, BLOCK), 1)
    ll = lax.broadcasted_iota(jnp.int32, (BLOCK, BLOCK, BLOCK), 2)
    pick = (ii - jj == ll).astype(jnp.float32).reshape(BLOCK * BLOCK, BLOCK)
    toeplitz = jnp.dot(pick, impulse, precision=lax.Precision.HIGHEST).reshape(BLOCK, BLOCK, width)
    tails = decay_in[::-1]
    heads = residues[None] * decay_in * jnp.exp(-rates)[None]
    shaped = values.reshape(blocks, BLOCK, width)
    inner = jnp.einsum("ijc,bjc->bic", toeplitz, shaped, precision=lax.Precision.HIGHEST)
    ends = jnp.einsum("jcm,bjc->bcm", tails, shaped, precision=lax.Precision.HIGHEST)
    factor = jnp.broadcast_to(jnp.exp(-BLOCK * rates)[None], ends.shape)
    states, _ = lax.associative_scan(link_states, (ends, factor))
    starts = jnp.concatenate([jnp.zeros_like(states[:1]), states[:-1]], axis=0)
    offsets = jnp.exp(-(BLOCK * jnp.arange(blocks, dtype=jnp.float32))[:, None, None] * rates[None])
    return (inner, starts, states[-1], heads, offsets)


def link_states(earlier, later):
    return (later[0] + later[1] * earlier[0], earlier[1] * later[1])


def finish(inner, starts, heads, values, skip):
    carried = jnp.einsum("icm,bcm->bic", heads, starts, precision=lax.Precision.HIGHEST)
    return (inner + carried).reshape(values.shape) + skip[None] * values


def gathered_tokens(tokens, lanes):
    rows, width = tokens.shape
    copies = jnp.broadcast_to(tokens[:, None], (rows, lanes // 2, width))
    chips = lax.all_to_all(copies, "cx", 1, 1)
    copies = jnp.broadcast_to(chips[:, None], (rows, 2, lanes // 2, width))
    return lax.all_to_all(copies, "core", 1, 1)


def scattered_terms(terms):
    pairs = lax.all_to_all(terms, "core", 0, 0)
    pairs = jnp.sum(pairs.astype(jnp.float32), axis=0).astype(jnp.bfloat16)
    parts = lax.all_to_all(pairs, "cx", 0, 0)
    return jnp.sum(parts.astype(jnp.float32), axis=0).astype(jnp.bfloat16)


def make_shards(count, lanes):
    def shards(tokens, in_weight, short_taps, rates, residues, skip, out_weight):
        rows = tokens.shape[0]
        width = in_weight.shape[2]
        whole = gathered_tokens(tokens, lanes)
        halo = passed_along(whole[rows - (SHORT - 1) :], CTX, count, 1)

        def across_yh(part):
            return lax.all_gather(part, "yh", axis=1)

        def across_z(part):
            part = lax.all_gather(part, "z", axis=2)
            return part.reshape(part.shape[0], -1, part.shape[-1])

        def shortened(weight):
            weight = weight.reshape(weight.shape[0], lanes // 2, 2, -1, weight.shape[-1])
            proj = jnp.einsum("toxd,jxodc->jtc", whole, weight, preferred_element_type=jnp.float32)
            earlier = jnp.einsum("toxd,jxodc->jtc", halo, weight, preferred_element_type=jnp.float32)
            proj = jnp.concatenate([earlier, proj], axis=1).astype(jnp.bfloat16)
            return proj.astype(jnp.float32)

        def filtered(widened, taps):
            feats = jnp.zeros((widened.shape[0], rows, width), jnp.float32)
            for i in range(SHORT):
                feats = feats + taps[i][:, None, :] * widened[:, SHORT - 1 - i : SHORT - 1 - i + rows, :]
            return feats

        streams = across_yh(in_weight)
        packed, streams = lax.optimization_barrier((out_weight, streams))
        streams = across_z(streams)
        packed = lax.all_gather(packed, "yh", axis=1)
        feats = filtered(shortened(streams), short_taps)
        packed = lax.all_gather(packed, "z", axis=2).reshape(width, -1)
        query = feats[0]
        feats = feats[1:]
        gated = (feats[0] * feats[1]).astype(jnp.bfloat16)
        values = gated.astype(jnp.float32)
        inner, starts, final, heads, offsets = block_terms(values, rates, residues)
        incoming = carried_in(final, rates, rows, count)
        starts = starts + offsets * incoming[None]
        conv = finish(inner, starts, heads, values, skip)
        hidden = (query * conv).astype(jnp.bfloat16)
        out_w = jnp.transpose(packed.reshape(width, lanes // 2, 2, -1), (0, 2, 1, 3))
        terms = jnp.einsum("tc,cyxe->yxte", hidden, out_w, preferred_element_type=jnp.float32)
        return scattered_terms(terms.astype(jnp.bfloat16))

    return shards


def solution(mesh):
    count = mesh.shape["ctx"]
    lanes = mesh.shape["ch"]
    fine = Mesh(mesh.devices.reshape(2, count // 2, lanes // 2, 2), CTX + CH)
    placed = (
        P(CTX, CH),
        P(None, CTX, CH),
        P(None, None, CH),
        P(CH, None),
        P(CH, None),
        P(CH),
        P(CH, CTX),
    )
    return jax.shard_map(
        make_shards(count, lanes), mesh=fine, in_specs=placed, out_specs=P(CTX, CH), check_vma=False
    )
```

```python
import jax
import jax.numpy as jnp
import numpy as np
from jax import lax
from jax.sharding import Mesh
from jax.sharding import PartitionSpec as P

SHORT = 3
BLOCK = 64
CTX = ("yh", "z")
CH = ("cx", "core")


def passed_along(block, axis, count, distance):
    route = [(i - distance, i) for i in range(count) if i - distance >= 0]
    return lax.ppermute(block, axis, route)


def carried_in(final, rates, rows, count):
    copies = jnp.broadcast_to(final[None], (count,) + final.shape)
    every = lax.all_to_all(copies, CTX, 0, 0)
    position = lax.axis_index(CTX)
    earlier = jnp.arange(count)
    gap = jnp.maximum(position - 1 - earlier, 0).astype(jnp.float32)
    weight = jnp.exp(-(gap[:, None, None] * rows) * rates[None])
    weight = jnp.where((earlier < position)[:, None, None], weight, 0.0)
    return jnp.sum(weight * every, axis=0)


def block_terms(values, rates, residues):
    length, width = values.shape
    blocks = length // BLOCK
    where_in = jnp.arange(BLOCK, dtype=jnp.float32)
    decay_in = jnp.exp(-where_in[:, None, None] * rates[None])
    impulse = jnp.sum(residues[None] * decay_in, axis=2)
    ii = lax.broadcasted_iota(jnp.int32, (BLOCK, BLOCK, BLOCK), 0)
    jj = lax.broadcasted_iota(jnp.int32, (BLOCK, BLOCK, BLOCK), 1)
    ll = lax.broadcasted_iota(jnp.int32, (BLOCK, BLOCK, BLOCK), 2)
    pick = (ii - jj == ll).astype(jnp.float32).reshape(BLOCK * BLOCK, BLOCK)
    toeplitz = jnp.dot(pick, impulse, precision=lax.Precision.HIGHEST).reshape(BLOCK, BLOCK, width)
    tails = decay_in[::-1]
    heads = residues[None] * decay_in * jnp.exp(-rates)[None]
    shaped = values.reshape(blocks, BLOCK, width)
    inner = jnp.einsum("ijc,bjc->bic", toeplitz, shaped, precision=lax.Precision.HIGHEST)
    ends = jnp.einsum("jcm,bjc->bcm", tails, shaped, precision=lax.Precision.HIGHEST)
    factor = jnp.broadcast_to(jnp.exp(-BLOCK * rates)[None], ends.shape)
    states, _ = lax.associative_scan(link_states, (ends, factor))
    starts = jnp.concatenate([jnp.zeros_like(states[:1]), states[:-1]], axis=0)
    offsets = jnp.exp(-(BLOCK * jnp.arange(blocks, dtype=jnp.float32))[:, None, None] * rates[None])
    return (inner, starts, states[-1], heads, offsets)


def link_states(earlier, later):
    return (later[0] + later[1] * earlier[0], earlier[1] * later[1])


def finish(inner, starts, heads, values, skip):
    carried = jnp.einsum("icm,bcm->bic", heads, starts, precision=lax.Precision.HIGHEST)
    return (inner + carried).reshape(values.shape) + skip[None] * values


def gathered_tokens(tokens, lanes):
    copies = jnp.broadcast_to(tokens[:, None], (tokens.shape[0], lanes, tokens.shape[1]))
    return lax.all_to_all(copies, CH, 1, 1)


def scattered_terms(terms):
    pairs = lax.all_to_all(terms, "core", 0, 0)
    pairs = jnp.sum(pairs.astype(jnp.float32), axis=0).astype(jnp.bfloat16)
    parts = lax.all_to_all(pairs, "cx", 0, 0)
    return jnp.sum(parts.astype(jnp.float32), axis=0).astype(jnp.bfloat16)


def make_shards(count, lanes):
    def shards(tokens, in_weight, short_taps, rates, residues, skip, out_weight):
        rows = tokens.shape[0]
        width = in_weight.shape[2]
        whole = gathered_tokens(tokens, lanes)
        halo = passed_along(whole[rows - (SHORT - 1) :], CTX, count, 1)

        def across_yh(part):
            return lax.all_gather(part, "yh", axis=1)

        def across_z(part):
            part = lax.all_gather(part, "z", axis=2)
            return part.reshape(part.shape[0], -1, part.shape[-1])

        def shortened(weight):
            weight = weight.reshape(weight.shape[0], lanes, -1, weight.shape[-1])
            proj = jnp.einsum("tkd,jkdc->jtc", whole, weight, preferred_element_type=jnp.float32)
            earlier = jnp.einsum("tkd,jkdc->jtc", halo, weight, preferred_element_type=jnp.float32)
            proj = jnp.concatenate([earlier, proj], axis=1).astype(jnp.bfloat16)
            return proj.astype(jnp.float32)

        def filtered(widened, taps):
            feats = jnp.zeros((widened.shape[0], rows, width), jnp.float32)
            for i in range(SHORT):
                feats = feats + taps[i][:, None, :] * widened[:, SHORT - 1 - i : SHORT - 1 - i + rows, :]
            return feats

        streams = across_yh(in_weight)
        packed, streams = lax.optimization_barrier((out_weight, streams))
        streams = across_z(streams)
        packed = lax.all_gather(packed, "yh", axis=1)
        feats = filtered(shortened(streams), short_taps)
        packed = lax.all_gather(packed, "z", axis=2).reshape(width, -1)
        query = feats[0]
        feats = feats[1:]
        gated = (feats[0] * feats[1]).astype(jnp.bfloat16)
        values = gated.astype(jnp.float32)
        inner, starts, final, heads, offsets = block_terms(values, rates, residues)
        incoming = carried_in(final, rates, rows, count)
        starts = starts + offsets * incoming[None]
        conv = finish(inner, starts, heads, values, skip)
        hidden = (query * conv).astype(jnp.bfloat16)
        out_w = packed.reshape(width, lanes // 2, 2, -1)
        terms = jnp.stack(
            [jnp.einsum("tc,cxe->xte", hidden, out_w[:, :, y], preferred_element_type=jnp.float32) for y in range(2)]
        )
        return scattered_terms(terms.astype(jnp.bfloat16))

    return shards


def solution(mesh):
    count = mesh.shape["ctx"]
    lanes = mesh.shape["ch"]
    fine = Mesh(mesh.devices.reshape(2, count // 2, lanes // 2, 2), CTX + CH)
    placed = (
        P(CTX, CH),
        P(None, CTX, CH),
        P(None, None, CH),
        P(CH, None),
        P(CH, None),
        P(CH),
        P(CH, CTX),
    )
    return jax.shard_map(
        make_shards(count, lanes), mesh=fine, in_specs=placed, out_specs=P(CTX, CH), check_vma=False
    )
```
